256 devices in a mesh: ctx: 32 (over x, y, core), tp: 8 (over z).
Axes of the slice: x: 4, y: 4, z: 8, core: 2. Of those that a mesh axis runs over, the one named last changes fastest.
Arguments:
- tokens: bfloat16 [8192, 4096], P('ctx'), may hold values from -700 to 700
- doc_lengths: int32 [64], replicated, may hold values from 1 to 4096, 8192 in all
- norm_gain: bfloat16 [4096], replicated, may hold values from 0.099609375 to 1.8984375
- w_query: bfloat16 [4096, 4096], P(None, 'tp'), may hold values from -3 to 3
- w_key: bfloat16 [4096, 1024], P(None, 'tp'), may hold values from -3 to 3
- w_value: bfloat16 [4096, 1024], P(None, 'tp'), may hold values from -0.09375 to 0.09375
- w_out: bfloat16 [4096, 4096], P('tp'), may hold values from -0.5 to 0.5
Outputs:
- mixed: bfloat16 [8192, 4096], P('ctx', 'tp')
The draws below stay inside these ranges and needn't reach their ends.
Inputs may be any that keep to these rules, and one draw needn't show every extreme that they name: `doc_lengths`: document lengths in packing order; they sum to 8192, and the longest has exactly 4096 tokens.
All inputs are finite; a program needn't handle non-finite values.
Results may differ from the reference program's by a relative error of at most 0.02.
The reference program's roundings to bfloat16 on the way count: a program that leaves them out, or rounds other values in their place, can miss the bound.
Values may be sent and summed in bfloat16 or wider, within the bound.
No kernel may reach another device: no remote copies, remote signals or barrier semaphores. Data moves between devices by JAX's collectives and lax.ppermute only.
A program may use at most 64 MiB of HBM per device.

```python
import math
import jax
import jax.numpy as jnp
import numpy as np
from jax import lax

D = 4096
HEADS = 32
KV_HEADS = 8
HEAD_DIM = 128
TOK_DEV = 256
SEQ = 8192
MOST = 4096
DOCS = 64
N_CTX = 32
N_TP = 8


def draw_w_query(key, part):
    drawn = jax.random.truncated_normal(jax.random.fold_in(key, 303), -4.0, 4.0, (D, HEADS * HEAD_DIM), jnp.float32) * (1.25 / math.sqrt(D))
    return drawn.astype(jnp.bfloat16)


def draw_w_key(key, part):
    drawn = jax.random.truncated_normal(jax.random.fold_in(key, 404), -4.0, 4.0, (D, KV_HEADS * HEAD_DIM), jnp.float32) * (1.25 / math.sqrt(D))
    return drawn.astype(jnp.bfloat16)


def draw_tokens(key, part):
    column_scale = jnp.exp(jax.random.uniform(jax.random.fold_in(key, 11), (D,), jnp.float32, 0.0, math.log(10.0)))
    drawn = jax.random.truncated_normal(jax.random.fold_in(key, 15), -4.0, 4.0, (SEQ, D), jnp.float32)
    row_scale = jnp.exp(jax.random.uniform(jax.random.fold_in(key, 16), (SEQ, 1), jnp.float32, 0.0, math.log(10.0)))
    result = drawn * row_scale
    return (result * column_scale[None, :]).astype(jnp.bfloat16)


def shard_levels(rng, dims, split, smallest, high):
    loudness, own = 1.0, jax.random.fold_in(rng, 6)
    for axis_at, parts in split:
        steps = jnp.exp(jax.random.uniform(jax.random.fold_in(own, axis_at), (parts,), jnp.float32, smallest / len(split), high / len(split)))
        loudness = loudness * jnp.repeat(steps, dims[axis_at] // parts).reshape([-1 if axis == axis_at else 1 for axis in range(len(dims))])
    return loudness


def profile(count, total, most, slope):
    loads = [(1 << 20) // math.isqrt(rank ** slope) + 1 for rank in range(2, count + 1)]
    surplus, counts = total - most - (count - 1), [1] * (count - 1)
    while surplus > 0:
        movable = [i for i in range(count - 1) if counts[i] < most]
        whole, remaining = sum([loads[i] for i in movable]), surplus
        for i in movable:
            extra = min(most - counts[i], max(1, remaining * loads[i] // whole), surplus)
            counts[i] = counts[i] + extra
            surplus = surplus - extra
    return np.array([most] + counts)


def uneven_parts(own_key, amount, total, limit, slope):
    if amount == 2:
        one = jax.random.randint(own_key, (), max(1, total - limit), min(limit, total - 1) + 1)
        return jnp.stack([one, total - one])
    tallies = jnp.asarray(profile(amount, total, limit, slope), jnp.int32)
    twos = (amount - 1) // 2
    donor, sink = tallies[1:1 + 2 * twos:2], tallies[2:2 + 2 * twos:2]
    margin = jnp.minimum(donor - 1, limit - sink)
    moved = jax.random.randint(jax.random.fold_in(own_key, 1), (twos,), 0, 1 << 20) % (margin + 1)
    tallies = tallies.at[1:1 + 2 * twos:2].set(donor - moved).at[2:2 + 2 * twos:2].set(sink + moved)
    return tallies[jax.random.permutation(jax.random.fold_in(own_key, 2), amount)]


def centred(rng, extent, deviation, most, shards=(), held_as=jnp.bfloat16):
    values = jax.random.normal(rng, extent, jnp.float32) * deviation
    if len(shards) > 0:
        values = shard_levels(rng, extent, shards, -0.22, 0.18) * values
    return jnp.clip(values, min=-most, max=most).astype(held_as)


def setup_inputs(seed: int = 0) -> dict:
    key_list = jax.random.split(jax.random.key(seed), 8)
    tokens = draw_tokens(jax.random.fold_in(key_list[7], 71), 0)
    doc_lengths = uneven_parts(key_list[1], DOCS, SEQ, MOST, 2).astype(jnp.int32)
    norm_gain = jnp.clip(1.0 + 0.18 * jax.random.normal(key_list[2], (D,), jnp.float32), 0.099609375, 1.8984375).astype(jnp.bfloat16)
    w_query = draw_w_query(jax.random.fold_in(key_list[7], 71), 0)
    w_key = draw_w_key(jax.random.fold_in(key_list[7], 71), 0)
    w_value = centred(key_list[5], (D, KV_HEADS * HEAD_DIM), D ** -0.5, 0.09375, ((1, 8),))
    w_out = centred(key_list[6], (HEADS * HEAD_DIM, D), HEAD_DIM ** -0.5, 0.5, ((0, 8),))
    return {"tokens": tokens, "doc_lengths": doc_lengths, "norm_gain": norm_gain, "w_query": w_query, "w_key": w_key, "w_value": w_value, "w_out": w_out}


NEGATIVE = -1e+30
ROPE_BASE = 500000.0
EPSILON = 1e-05

def doc_starts(doc_lengths):
    ends = jnp.cumsum(doc_lengths).astype(jnp.int32)
    return (ends - doc_lengths).astype(jnp.int32)

def seg_info(positions, starts):
    inside = starts[None, :] <= positions[:, None]
    segment = lax.optimization_barrier(jnp.sum(inside.astype(jnp.int32), axis=1)) - 1
    doc_first = lax.optimization_barrier(jnp.max(jnp.where(inside, starts[None, :], 0), axis=1))
    return (segment.astype(jnp.int32), doc_first.astype(jnp.int32))

def rotate(lifted, offsets):
    halfway = lifted.shape[-1] // 2
    fraction = jnp.arange(halfway, dtype=jnp.float32) * (2.0 / lifted.shape[-1])
    inverse = jnp.exp(-jnp.log(jnp.float32(ROPE_BASE)) * fraction)
    angles = offsets.astype(jnp.float32)[:, None] * inverse[None, :]
    cosine = jnp.cos(angles)[:, None, :]
    sine_table = jnp.sin(angles)[:, None, :]
    leading = lifted[..., :halfway]
    trailing = lifted[..., halfway:]
    return jnp.concatenate([leading * cosine - trailing * sine_table, trailing * cosine + leading * sine_table], axis=-1)

def normalize(tokens, norm_gain):
    widened = tokens.astype(jnp.float32)
    square = lax.optimization_barrier(jnp.mean(widened * widened, axis=-1, keepdims=True))
    return (widened * lax.rsqrt(square + EPSILON) * norm_gain.astype(jnp.float32)).astype(jnp.bfloat16)

def project(normed, weight, offsets):
    head_count = weight.shape[1] // HEAD_DIM
    lifted = jnp.dot(normed, weight, preferred_element_type=jnp.float32)
    lifted = lifted.reshape(normed.shape[0], head_count, HEAD_DIM)
    return lax.optimization_barrier(rotate(lifted, offsets).astype(jnp.bfloat16))

def block_terms(query_block, key_block, value_block, allowed):
    scores = jnp.einsum('tkgd,skd->kgts', query_block.astype(jnp.float32), key_block.astype(jnp.float32)) * HEAD_DIM ** (-0.5)
    scores = jnp.where(allowed[None, None], scores, NEGATIVE)
    highest = lax.optimization_barrier(jnp.max(scores, axis=-1))
    weights = jnp.where(allowed[None, None], jnp.exp(scores - highest[..., None]), 0.0).astype(jnp.bfloat16)
    weights = lax.optimization_barrier(weights).astype(jnp.float32)
    numerator = jnp.einsum('kgts,skd->tkgd', weights, value_block.astype(jnp.float32))
    denominator = lax.optimization_barrier(jnp.sum(weights, axis=-1))
    return (highest, numerator, denominator)

def combine(carried, terms):
    highest, numerator, denominator = carried
    block_high, block_num, block_den = terms
    summit = jnp.maximum(highest, block_high)
    retain = jnp.exp(highest - summit)
    admit = jnp.exp(block_high - summit)
    numerator = numerator * jnp.transpose(retain, (2, 0, 1))[..., None] + block_num * jnp.transpose(admit, (2, 0, 1))[..., None]
    denominator = denominator * retain + block_den * admit
    return (summit, numerator, denominator)

def finish(carried):
    numerator = carried[1]
    denominator = jnp.transpose(carried[2], (2, 0, 1))[..., None]
    result = (numerator / denominator).astype(jnp.bfloat16)
    return result.reshape(numerator.shape[0], -1)

def reference(tokens, doc_lengths, norm_gain, w_query, w_key, w_value, w_out):
    sharing = HEADS // KV_HEADS
    starts = doc_starts(doc_lengths)
    everywhere = jnp.arange(SEQ, dtype=jnp.int32)
    segment, doc_first = seg_info(everywhere, starts)
    offsets = everywhere - doc_first
    normed = normalize(tokens, norm_gain)
    queries = project(normed, w_query, offsets).reshape(SEQ, KV_HEADS, sharing, HEAD_DIM)
    keys = project(normed, w_key, offsets)
    values = jnp.dot(normed, w_value, preferred_element_type=jnp.float32).astype(jnp.bfloat16)
    values = values.reshape(SEQ, KV_HEADS, HEAD_DIM)

    def one_block(block_number):
        row_start = (block_number * TOK_DEV).astype(jnp.int32)
        query_block = lax.dynamic_slice_in_dim(queries, row_start, TOK_DEV, 0)
        query_segments = lax.dynamic_slice_in_dim(segment, row_start, TOK_DEV, 0)
        query_places = row_start + jnp.arange(TOK_DEV, dtype=jnp.int32)
        lowest = lax.dynamic_index_in_dim(doc_first, row_start, 0, keepdims=False)
        initial = (jnp.full((KV_HEADS, sharing, TOK_DEV), NEGATIVE, jnp.float32), jnp.zeros((TOK_DEV, KV_HEADS, sharing, HEAD_DIM), jnp.float32), jnp.zeros((KV_HEADS, sharing, TOK_DEV), jnp.float32))

        def absorb_block(key_number, carried):
            key_start = (key_number * TOK_DEV).astype(jnp.int32)

            def include(state):
                key_places = key_start + jnp.arange(TOK_DEV, dtype=jnp.int32)
                key_segments = lax.dynamic_slice_in_dim(segment, key_start, TOK_DEV, 0)
                allowed = (key_segments[None, :] == query_segments[:, None]) & (key_places[None, :] <= query_places[:, None])
                key_block = lax.dynamic_slice_in_dim(keys, key_start, TOK_DEV, 0)
                value_block = lax.dynamic_slice_in_dim(values, key_start, TOK_DEV, 0)
                return combine(state, block_terms(query_block, key_block, value_block, allowed))
            useful = key_start + TOK_DEV - 1 >= lowest
            return lax.cond(useful, include, lambda state: state, carried)
        return finish(lax.fori_loop(0, block_number + 1, absorb_block, initial))
    attended = lax.map(one_block, jnp.arange(N_CTX, dtype=jnp.int32)).reshape(SEQ, HEADS * HEAD_DIM)
    group_width = HEADS // N_TP * HEAD_DIM
    running_sum = jnp.zeros((SEQ, D), jnp.float32)
    for group_number in range(N_TP):
        lower = group_number * group_width
        group_sum = jnp.dot(attended[:, lower:lower + group_width], w_out[lower:lower + group_width], preferred_element_type=jnp.float32).astype(jnp.bfloat16)
        group_sum = lax.optimization_barrier(group_sum)
        running_sum = running_sum + group_sum.astype(jnp.float32)
    return running_sum.astype(jnp.bfloat16)
```

```python
import functools

import jax
import jax.numpy as jnp
from jax import lax
from jax.experimental import pallas as pl
from jax.experimental.pallas import tpu as pltpu
from jax.sharding import PartitionSpec as P

HEAD_DIM = 128
MOST = 4096


NEGATIVE = -1e30
ROPE_BASE = 500000.0
EPSILON = 1e-05


def doc_starts(doc_lengths):
    ends = jnp.cumsum(doc_lengths)
    return ends - doc_lengths


def seg_info(positions, starts):
    inside = starts[None, :] <= positions[:, None]
    segment = jnp.sum(inside.astype(jnp.int32), axis=1) - 1
    doc_first = jnp.max(jnp.where(inside, starts[None, :], 0), axis=1)
    return (segment, doc_first)


def rotate(lifted, offsets):
    halfway = lifted.shape[-1] // 2
    fraction = jnp.arange(halfway, dtype=jnp.float32) * (2.0 / lifted.shape[-1])
    inverse = jnp.exp(-jnp.log(jnp.float32(ROPE_BASE)) * fraction)
    angles = offsets.astype(jnp.float32)[:, None] * inverse[None, :]
    cosine = jnp.cos(angles)[:, None, :]
    sine_table = jnp.sin(angles)[:, None, :]
    leading = lifted[..., :halfway]
    trailing = lifted[..., halfway:]
    return jnp.concatenate(
        [leading * cosine - trailing * sine_table, trailing * cosine + leading * sine_table],
        axis=-1,
    )


def normalize(tokens, norm_gain):
    widened = tokens.astype(jnp.float32)
    square = jnp.mean(widened * widened, axis=-1, keepdims=True)
    return (widened * lax.rsqrt(square + EPSILON) * norm_gain.astype(jnp.float32)).astype(
        jnp.bfloat16
    )


def project(normed, weight, offsets):
    head_count = weight.shape[1] // HEAD_DIM
    lifted = jnp.dot(normed, weight, preferred_element_type=jnp.float32)
    lifted = lifted.reshape(normed.shape[0], head_count, HEAD_DIM)
    return rotate(lifted, offsets).astype(jnp.bfloat16)


def flash_kernel(bounds, q_ref, kv_ref, kseg_ref, qseg_ref, o_ref, m_sc, l_sc, acc_sc, *, heads):
    step = pl.program_id(0)
    first = bounds[0]
    own = bounds[1]
    block = first + step
    rows = q_ref.shape[0]

    @pl.when(step == 0)
    def _():
        m_sc[...] = jnp.full(m_sc.shape, NEGATIVE, jnp.float32)
        l_sc[...] = jnp.zeros(l_sc.shape, jnp.float32)
        acc_sc[...] = jnp.zeros(acc_sc.shape, jnp.float32)

    @pl.when(block <= own)
    def _():
        keys = kv_ref[0]
        values = kv_ref[1]
        query_places = own * rows + lax.broadcasted_iota(jnp.int32, (rows, rows), 0)
        key_places = block * rows + lax.broadcasted_iota(jnp.int32, (rows, rows), 1)
        allowed = (qseg_ref[...] == kseg_ref[...]) & (key_places <= query_places)
        for h in range(heads):
            query = q_ref[:, h * HEAD_DIM:(h + 1) * HEAD_DIM]
            scores = lax.dot_general(
                query, keys, (((1,), (1,)), ((), ())), preferred_element_type=jnp.float32
            ) * HEAD_DIM ** (-0.5)
            scores = jnp.where(allowed, scores, NEGATIVE)
            highest = jnp.max(scores, axis=1, keepdims=True)
            weights = jnp.where(allowed, jnp.exp(scores - highest), 0.0).astype(jnp.bfloat16)
            numerator = jnp.dot(weights, values, preferred_element_type=jnp.float32)
            denominator = jnp.sum(weights.astype(jnp.float32), axis=1, keepdims=True)
            previous = m_sc[h]
            summit = jnp.maximum(previous, highest)
            retain = jnp.exp(previous - summit)
            admit = jnp.exp(highest - summit)
            acc_sc[h] = acc_sc[h] * retain + numerator * admit
            l_sc[h] = l_sc[h] * retain + denominator * admit
            m_sc[h] = summit

    @pl.when(step == pl.num_programs(0) - 1)
    def _():
        for h in range(heads):
            o_ref[:, h * HEAD_DIM:(h + 1) * HEAD_DIM] = (acc_sc[h] / l_sc[h]).astype(o_ref.dtype)


def flash(bounds, queries, gathered, key_segments, query_segments, steps):
    rows, width = queries.shape
    heads = width // HEAD_DIM

    def kv_map(step, b):
        return (0, jnp.minimum(b[0] + step, b[1]), 0)

    def kseg_map(step, b):
        return (0, jnp.minimum(b[0] + step, b[1]))

    grid_spec = pltpu.PrefetchScalarGridSpec(
        num_scalar_prefetch=1,
        grid=(steps,),
        in_specs=[
            pl.BlockSpec((rows, width), lambda step, b: (0, 0)),
            pl.BlockSpec((2, rows, HEAD_DIM), kv_map),
            pl.BlockSpec((1, rows), kseg_map),
            pl.BlockSpec((rows, 1), lambda step, b: (0, 0)),
        ],
        out_specs=pl.BlockSpec((rows, width), lambda step, b: (0, 0)),
        scratch_shapes=[
            pltpu.VMEM((heads, rows, 1), jnp.float32),
            pltpu.VMEM((heads, rows, 1), jnp.float32),
            pltpu.VMEM((heads, rows, HEAD_DIM), jnp.float32),
        ],
    )
    return pl.pallas_call(
        functools.partial(flash_kernel, heads=heads),
        grid_spec=grid_spec,
        out_shape=jax.ShapeDtypeStruct((rows, width), jnp.bfloat16),
    )(bounds, queries, gathered, key_segments, query_segments)


def on_device(tokens, doc_lengths, norm_gain, w_query, w_key, w_value, w_out):
    shard_rows = tokens.shape[0]
    ctx_count = lax.axis_size("ctx")
    ctx_place = lax.axis_index("ctx")
    starts = doc_starts(doc_lengths)
    local_places = jnp.arange(shard_rows, dtype=jnp.int32)
    positions = ctx_place * shard_rows + local_places
    segment, doc_first = seg_info(positions, starts)
    every_place = jnp.arange(shard_rows * ctx_count, dtype=jnp.int32)
    every_segment, unused_first = seg_info(every_place, starts)
    normed = normalize(tokens, norm_gain)
    offsets = positions - doc_first
    queries = project(normed, w_query, offsets).reshape(shard_rows, -1)
    keys = project(normed, w_key, offsets).reshape(shard_rows, -1)
    values = jnp.dot(normed, w_value, preferred_element_type=jnp.float32).astype(jnp.bfloat16)
    packed = jnp.stack([keys, values])
    gathered = lax.all_gather(packed, "ctx", axis=1, tiled=True)
    bounds = jnp.stack([doc_first[0] // shard_rows, ctx_place]).astype(jnp.int32)
    steps = min(ctx_count, -(-(MOST - 1) // shard_rows) + 1)
    attended = flash(
        bounds,
        queries,
        gathered,
        every_segment.reshape(1, -1).astype(jnp.int32),
        segment.reshape(-1, 1).astype(jnp.int32),
        steps,
    )
    partial_value = jnp.dot(attended, w_out, preferred_element_type=jnp.float32)
    summed = lax.psum_scatter(
        partial_value.astype(jnp.bfloat16), "tp", scatter_dimension=1, tiled=True
    )
    return summed


def solution(mesh):
    placed = (P("ctx", None), P(), P(), P(None, "tp"), P(None, "tp"), P(None, "tp"), P("tp", None))
    return jax.shard_map(
        on_device, mesh=mesh, in_specs=placed, out_specs=P("ctx", "tp"), check_vma=False
    )
```

```python
import functools

import jax
import jax.numpy as jnp
from jax import lax
from jax.experimental import pallas as pl
from jax.experimental.pallas import tpu as pltpu
from jax.sharding import PartitionSpec as P

HEAD_DIM = 128
MOST = 4096


NEGATIVE = -1e30
ROPE_BASE = 500000.0
EPSILON = 1e-05


def doc_starts(doc_lengths):
    ends = jnp.cumsum(doc_lengths)
    return ends - doc_lengths


def seg_info(positions, starts):
    inside = starts[None, :] <= positions[:, None]
    segment = jnp.sum(inside.astype(jnp.int32), axis=1) - 1
    doc_first = jnp.max(jnp.where(inside, starts[None, :], 0), axis=1)
    return (segment, doc_first)


def rotate(lifted, offsets):
    halfway = lifted.shape[-1] // 2
    fraction = jnp.arange(halfway, dtype=jnp.float32) * (2.0 / lifted.shape[-1])
    inverse = jnp.exp(-jnp.log(jnp.float32(ROPE_BASE)) * fraction)
    angles = offsets.astype(jnp.float32)[:, None] * inverse[None, :]
    cosine = jnp.cos(angles)[:, None, :]
    sine_table = jnp.sin(angles)[:, None, :]
    leading = lifted[..., :halfway]
    trailing = lifted[..., halfway:]
    return jnp.concatenate(
        [leading * cosine - trailing * sine_table, trailing * cosine + leading * sine_table],
        axis=-1,
    )


def normalize(tokens, norm_gain):
    widened = tokens.astype(jnp.float32)
    square = jnp.mean(widened * widened, axis=-1, keepdims=True)
    return (widened * lax.rsqrt(square + EPSILON) * norm_gain.astype(jnp.float32)).astype(
        jnp.bfloat16
    )


def project(normed, weight, offsets):
    head_count = weight.shape[1] // HEAD_DIM
    lifted = jnp.dot(normed, weight, preferred_element_type=jnp.float32)
    lifted = lifted.reshape(normed.shape[0], head_count, HEAD_DIM)
    return rotate(lifted, offsets).astype(jnp.bfloat16)


def flash_kernel(bounds, q_ref, kv_ref, kseg_ref, qseg_ref, o_ref, m_sc, l_sc, acc_sc, *, heads):
    step = pl.program_id(0)
    first = bounds[0]
    own = bounds[1]
    block = first + step
    rows = q_ref.shape[0]

    @pl.when(step == 0)
    def _():
        m_sc[...] = jnp.full(m_sc.shape, NEGATIVE, jnp.float32)
        l_sc[...] = jnp.zeros(l_sc.shape, jnp.float32)
        acc_sc[...] = jnp.zeros(acc_sc.shape, jnp.float32)

    @pl.when(block <= own)
    def _():
        keys = kv_ref[0]
        values = kv_ref[1]
        query_places = own * rows + lax.broadcasted_iota(jnp.int32, (rows, rows), 0)
        key_places = block * rows + lax.broadcasted_iota(jnp.int32, (rows, rows), 1)
        allowed = (qseg_ref[...] == kseg_ref[...]) & (key_places <= query_places)
        for h in range(heads):
            query = q_ref[:, h * HEAD_DIM:(h + 1) * HEAD_DIM]
            scores = lax.dot_general(
                query, keys, (((1,), (1,)), ((), ())), preferred_element_type=jnp.float32
            ) * HEAD_DIM ** (-0.5)
            scores = jnp.where(allowed, scores, NEGATIVE)
            highest = jnp.max(scores, axis=1, keepdims=True)
            weights = jnp.where(allowed, jnp.exp(scores - highest), 0.0).astype(jnp.bfloat16)
            numerator = jnp.dot(weights, values, preferred_element_type=jnp.float32)
            denominator = jnp.sum(weights.astype(jnp.float32), axis=1, keepdims=True)
            previous = m_sc[h]
            summit = jnp.maximum(previous, highest)
            retain = jnp.exp(previous - summit)
            admit = jnp.exp(highest - summit)
            acc_sc[h] = acc_sc[h] * retain + numerator * admit
            l_sc[h] = l_sc[h] * retain + denominator * admit
            m_sc[h] = summit

    @pl.when(step == pl.num_programs(0) - 1)
    def _():
        for h in range(heads):
            o_ref[:, h * HEAD_DIM:(h + 1) * HEAD_DIM] = (acc_sc[h] / l_sc[h]).astype(o_ref.dtype)


def flash(bounds, queries, gathered, key_segments, query_segments, steps):
    rows, width = queries.shape
    heads = width // HEAD_DIM

    def kv_map(step, b):
        return (0, jnp.minimum(b[0] + step, b[1]), 0)

    def kseg_map(step, b):
        return (0, jnp.minimum(b[0] + step, b[1]))

    grid_spec = pltpu.PrefetchScalarGridSpec(
        num_scalar_prefetch=1,
        grid=(steps,),
        in_specs=[
            pl.BlockSpec((rows, width), lambda step, b: (0, 0)),
            pl.BlockSpec((2, rows, HEAD_DIM), kv_map),
            pl.BlockSpec((1, rows), kseg_map),
            pl.BlockSpec((rows, 1), lambda step, b: (0, 0)),
        ],
        out_specs=pl.BlockSpec((rows, width), lambda step, b: (0, 0)),
        scratch_shapes=[
            pltpu.VMEM((heads, rows, 1), jnp.float32),
            pltpu.VMEM((heads, rows, 1), jnp.float32),
            pltpu.VMEM((heads, rows, HEAD_DIM), jnp.float32),
        ],
    )
    return pl.pallas_call(
        functools.partial(flash_kernel, heads=heads),
        grid_spec=grid_spec,
        out_shape=jax.ShapeDtypeStruct((rows, width), jnp.bfloat16),
    )(bounds, queries, gathered, key_segments, query_segments)


def on_device(tokens, doc_lengths, norm_gain, w_query, w_key, w_value, w_out):
    shard_rows = tokens.shape[0]
    ctx_count = lax.axis_size("ctx")
    ctx_place = lax.axis_index("ctx")
    starts = doc_starts(doc_lengths)
    local_places = jnp.arange(shard_rows, dtype=jnp.int32)
    positions = ctx_place * shard_rows + local_places
    segment, doc_first = seg_info(positions, starts)
    every_place = jnp.arange(shard_rows * ctx_count, dtype=jnp.int32)
    every_segment, unused_first = seg_info(every_place, starts)
    normed = normalize(tokens, norm_gain)
    offsets = positions - doc_first
    queries = project(normed, w_query, offsets).reshape(shard_rows, -1)
    keys = project(normed, w_key, offsets).reshape(shard_rows, -1)
    values = jnp.dot(normed, w_value, preferred_element_type=jnp.float32).astype(jnp.bfloat16)
    packed = jnp.stack([keys, values])
    gathered = lax.all_gather(packed, "ctx", axis=1, tiled=True)
    bounds = jnp.stack([doc_first[0] // shard_rows, ctx_place]).astype(jnp.int32)
    steps = min(ctx_count, -(-(MOST - 1) // shard_rows) + 1)
    attended = flash(
        bounds,
        queries,
        gathered,
        every_segment.reshape(1, -1).astype(jnp.int32),
        segment.reshape(-1, 1).astype(jnp.int32),
        steps,
    )
    partial_value = jnp.dot(attended, w_out, preferred_element_type=jnp.float32)
    return scatter_sum(partial_value.astype(jnp.bfloat16), "tp")


def scatter_sum(partial_value, axis):
    count = lax.axis_size(axis)
    place = lax.axis_index(axis)
    chunks = partial_value.reshape(partial_value.shape[0], count, -1)
    rightward = [(i, (i + 1) % count) for i in range(count)]
    leftward = [(i, (i - 1) % count) for i in range(count)]

    def pick(index):
        return lax.dynamic_index_in_dim(chunks, index % count, axis=1, keepdims=False).astype(
            jnp.float32
        )

    reach_right = count // 2
    reach_left = count - 1 - reach_right
    from_left = pick(place + reach_right)
    from_right = pick(place - reach_left)
    for hop in range(1, reach_right + 1):
        from_left = lax.ppermute(from_left.astype(jnp.bfloat16), axis, rightward).astype(jnp.float32)
        if hop <= reach_left:
            from_right = lax.ppermute(from_right.astype(jnp.bfloat16), axis, leftward).astype(
                jnp.float32
            )
        if hop < reach_right:
            from_left = from_left + pick(place + reach_right - hop)
        if hop < reach_left:
            from_right = from_right + pick(place - reach_left + hop)
    return (from_left + from_right + pick(place)).astype(jnp.bfloat16)


def solution(mesh):
    placed = (P("ctx", None), P(), P(), P(None, "tp"), P(None, "tp"), P(None, "tp"), P("tp", None))
    return jax.shard_map(
        on_device, mesh=mesh, in_specs=placed, out_specs=P("ctx", "tp"), check_vma=False
    )
```

```python
import functools

import jax
import jax.numpy as jnp
from jax import lax
from jax.experimental import pallas as pl
from jax.experimental.pallas import tpu as pltpu
from jax.sharding import PartitionSpec as P

HEAD_DIM = 128
MOST = 4096


NEGATIVE = -1e30
ROPE_BASE = 500000.0
EPSILON = 1e-05


def doc_starts(doc_lengths):
    ends = jnp.cumsum(doc_lengths)
    return ends - doc_lengths


def seg_info(positions, starts):
    inside = starts[None, :] <= positions[:, None]
    segment = jnp.sum(inside.astype(jnp.int32), axis=1) - 1
    doc_first = jnp.max(jnp.where(inside, starts[None, :], 0), axis=1)
    return (segment, doc_first)


def rotate(lifted, offsets):
    halfway = lifted.shape[-1] // 2
    fraction = jnp.arange(halfway, dtype=jnp.float32) * (2.0 / lifted.shape[-1])
    inverse = jnp.exp(-jnp.log(jnp.float32(ROPE_BASE)) * fraction)
    angles = offsets.astype(jnp.float32)[:, None] * inverse[None, :]
    cosine = jnp.cos(angles)[:, None, :]
    sine_table = jnp.sin(angles)[:, None, :]
    leading = lifted[..., :halfway]
    trailing = lifted[..., halfway:]
    return jnp.concatenate(
        [leading * cosine - trailing * sine_table, trailing * cosine + leading * sine_table],
        axis=-1,
    )


def normalize(tokens, norm_gain):
    widened = tokens.astype(jnp.float32)
    square = jnp.mean(widened * widened, axis=-1, keepdims=True)
    return (widened * lax.rsqrt(square + EPSILON) * norm_gain.astype(jnp.float32)).astype(
        jnp.bfloat16
    )


def project(normed, weight, offsets):
    head_count = weight.shape[1] // HEAD_DIM
    lifted = jnp.dot(normed, weight, preferred_element_type=jnp.float32)
    lifted = lifted.reshape(normed.shape[0], head_count, HEAD_DIM)
    return rotate(lifted, offsets).astype(jnp.bfloat16)


def flash_kernel(bounds, q_ref, kv_ref, kseg_ref, qseg_ref, o_ref, m_sc, l_sc, acc_sc, *, heads):
    step = pl.program_id(0)
    first = bounds[0]
    own = bounds[1]
    block = first + step
    rows = q_ref.shape[0]

    @pl.when(step == 0)
    def _():
        m_sc[...] = jnp.full(m_sc.shape, NEGATIVE, jnp.float32)
        l_sc[...] = jnp.zeros(l_sc.shape, jnp.float32)
        acc_sc[...] = jnp.zeros(acc_sc.shape, jnp.float32)

    @pl.when(block <= own)
    def _():
        keys = kv_ref[0]
        values = kv_ref[1]
        query_places = own * rows + lax.broadcasted_iota(jnp.int32, (rows, rows), 0)
        key_places = block * rows + lax.broadcasted_iota(jnp.int32, (rows, rows), 1)
        allowed = (qseg_ref[...] == kseg_ref[...]) & (key_places <= query_places)
        for h in range(heads):
            query = q_ref[:, h * HEAD_DIM:(h + 1) * HEAD_DIM]
            scores = lax.dot_general(
                query, keys, (((1,), (1,)), ((), ())), preferred_element_type=jnp.float32
            ) * HEAD_DIM ** (-0.5)
            scores = jnp.where(allowed, scores, NEGATIVE)
            highest = jnp.max(scores, axis=1, keepdims=True)
            weights = jnp.where(allowed, jnp.exp(scores - highest), 0.0).astype(jnp.bfloat16)
            numerator = jnp.dot(weights, values, preferred_element_type=jnp.float32)
            denominator = jnp.sum(weights.astype(jnp.float32), axis=1, keepdims=True)
            previous = m_sc[h]
            summit = jnp.maximum(previous, highest)
            retain = jnp.exp(previous - summit)
            admit = jnp.exp(highest - summit)
            acc_sc[h] = acc_sc[h] * retain + numerator * admit
            l_sc[h] = l_sc[h] * retain + denominator * admit
            m_sc[h] = summit

    @pl.when(step == pl.num_programs(0) - 1)
    def _():
        for h in range(heads):
            o_ref[:, h * HEAD_DIM:(h + 1) * HEAD_DIM] = (acc_sc[h] / l_sc[h]).astype(o_ref.dtype)


def flash(bounds, queries, gathered, key_segments, query_segments, steps):
    rows, width = queries.shape
    heads = width // HEAD_DIM

    def kv_map(step, b):
        return (jnp.minimum(b[0] + step, b[1]) - b[1] + steps - 1, 0, 0, 0)

    def kseg_map(step, b):
        return (0, jnp.minimum(b[0] + step, b[1]))

    grid_spec = pltpu.PrefetchScalarGridSpec(
        num_scalar_prefetch=1,
        grid=(steps,),
        in_specs=[
            pl.BlockSpec((rows, width), lambda step, b: (0, 0)),
            pl.BlockSpec((None, 2, rows, HEAD_DIM), kv_map),
            pl.BlockSpec((1, rows), kseg_map),
            pl.BlockSpec((rows, 1), lambda step, b: (0, 0)),
        ],
        out_specs=pl.BlockSpec((rows, width), lambda step, b: (0, 0)),
        scratch_shapes=[
            pltpu.VMEM((heads, rows, 1), jnp.float32),
            pltpu.VMEM((heads, rows, 1), jnp.float32),
            pltpu.VMEM((heads, rows, HEAD_DIM), jnp.float32),
        ],
    )
    return pl.pallas_call(
        functools.partial(flash_kernel, heads=heads),
        grid_spec=grid_spec,
        out_shape=jax.ShapeDtypeStruct((rows, width), jnp.bfloat16),
    )(bounds, queries, gathered, key_segments, query_segments)


def steps_needed(shard_rows, ctx_count):
    return min(ctx_count, -(-(MOST - 1) // shard_rows) + 1)


def earlier_blocks(packed, axis, span):
    count = lax.axis_size(axis)
    place = lax.axis_index(axis)
    reach = span // 2
    chain = [packed]
    for k in range(1, reach + 1):
        pairs = [(i, i + 2 * k) for i in range(count - 2 * k)]
        chain.append(lax.ppermute(packed, axis, pairs))
    own = jnp.stack(chain)
    sibling = lax.ppermute(own, axis, [(i, i ^ 1) for i in range(count)])
    backward = sibling[::-1]
    odd = jnp.where(place % 2 == 0, backward[0:reach], backward[1:reach + 1])
    even = own[::-1]
    window = jnp.stack([even[:reach], odd], axis=1).reshape((2 * reach,) + packed.shape)
    return jnp.concatenate([window, own[:1]], 0)


def on_device(tokens, doc_lengths, norm_gain, w_query, w_key, w_value, w_out):
    shard_rows = tokens.shape[0]
    ctx_count = lax.axis_size("ctx")
    ctx_place = lax.axis_index("ctx")
    starts = doc_starts(doc_lengths)
    local_places = jnp.arange(shard_rows, dtype=jnp.int32)
    positions = ctx_place * shard_rows + local_places
    segment, doc_first = seg_info(positions, starts)
    every_place = jnp.arange(shard_rows * ctx_count, dtype=jnp.int32)
    every_segment, unused_first = seg_info(every_place, starts)
    normed = normalize(tokens, norm_gain)
    offsets = positions - doc_first
    queries = project(normed, w_query, offsets).reshape(shard_rows, -1)
    keys = project(normed, w_key, offsets).reshape(shard_rows, -1)
    values = jnp.dot(normed, w_value, preferred_element_type=jnp.float32).astype(jnp.bfloat16)
    packed = jnp.stack([keys, values])
    gathered = earlier_blocks(packed, "ctx", steps_needed(shard_rows, ctx_count))
    bounds = jnp.stack([doc_first[0] // shard_rows, ctx_place]).astype(jnp.int32)
    steps = steps_needed(shard_rows, ctx_count)
    attended = flash(
        bounds,
        queries,
        gathered,
        every_segment.reshape(1, -1).astype(jnp.int32),
        segment.reshape(-1, 1).astype(jnp.int32),
        steps,
    )
    partial_value = jnp.dot(attended, w_out, preferred_element_type=jnp.float32)
    return scatter_sum(partial_value.astype(jnp.bfloat16), "tp")


def scatter_sum(partial_value, axis):
    count = lax.axis_size(axis)
    place = lax.axis_index(axis)
    chunks = partial_value.reshape(partial_value.shape[0], count, -1)
    rightward = [(i, (i + 1) % count) for i in range(count)]
    leftward = [(i, (i - 1) % count) for i in range(count)]

    def pick(index):
        return lax.dynamic_index_in_dim(chunks, index % count, axis=1, keepdims=False).astype(
            jnp.float32
        )

    reach_right = count // 2
    reach_left = count - 1 - reach_right
    from_left = pick(place + reach_right)
    from_right = pick(place - reach_left)
    for hop in range(1, reach_right + 1):
        from_left = lax.ppermute(from_left.astype(jnp.bfloat16), axis, rightward).astype(jnp.float32)
        if hop <= reach_left:
            from_right = lax.ppermute(from_right.astype(jnp.bfloat16), axis, leftward).astype(
                jnp.float32
            )
        if hop < reach_right:
            from_left = from_left + pick(place + reach_right - hop)
        if hop < reach_left:
            from_right = from_right + pick(place - reach_left + hop)
    return (from_left + from_right + pick(place)).astype(jnp.bfloat16)


def solution(mesh):
    placed = (P("ctx", None), P(), P(), P(None, "tp"), P(None, "tp"), P(None, "tp"), P("tp", None))
    return jax.shard_map(
        on_device, mesh=mesh, in_specs=placed, out_specs=P("ctx", "tp"), check_vma=False
    )
```

```python
import functools

import jax
import jax.numpy as jnp
from jax import lax
from jax.experimental import pallas as pl
from jax.experimental.pallas import tpu as pltpu
from jax.sharding import PartitionSpec as P

HEAD_DIM = 128
MOST = 4096


NEGATIVE = -1e30
ROPE_BASE = 500000.0
EPSILON = 1e-05


def doc_starts(doc_lengths):
    ends = jnp.cumsum(doc_lengths)
    return ends - doc_lengths


def seg_info(positions, starts):
    inside = starts[None, :] <= positions[:, None]
    segment = jnp.sum(inside.astype(jnp.int32), axis=1) - 1
    doc_first = jnp.max(jnp.where(inside, starts[None, :], 0), axis=1)
    return (segment, doc_first)


def rotate(lifted, offsets):
    halfway = lifted.shape[-1] // 2
    fraction = jnp.arange(halfway, dtype=jnp.float32) * (2.0 / lifted.shape[-1])
    inverse = jnp.exp(-jnp.log(jnp.float32(ROPE_BASE)) * fraction)
    angles = offsets.astype(jnp.float32)[:, None] * inverse[None, :]
    cosine = jnp.cos(angles)[:, None, :]
    sine_table = jnp.sin(angles)[:, None, :]
    leading = lifted[..., :halfway]
    trailing = lifted[..., halfway:]
    return jnp.concatenate(
        [leading * cosine - trailing * sine_table, trailing * cosine + leading * sine_table],
        axis=-1,
    )


def normalize(tokens, norm_gain):
    widened = tokens.astype(jnp.float32)
    square = jnp.mean(widened * widened, axis=-1, keepdims=True)
    return (widened * lax.rsqrt(square + EPSILON) * norm_gain.astype(jnp.float32)).astype(
        jnp.bfloat16
    )


def project(normed, weight, offsets):
    head_count = weight.shape[1] // HEAD_DIM
    lifted = jnp.dot(normed, weight, preferred_element_type=jnp.float32)
    lifted = lifted.reshape(normed.shape[0], head_count, HEAD_DIM)
    return rotate(lifted, offsets).astype(jnp.bfloat16)


def flash_kernel(bounds, kinds, q_ref, kv_ref, kseg_ref, qseg_ref, o_ref, m_sc, l_sc, acc_sc, *, heads):
    step = pl.program_id(0)
    first = bounds[0]
    own = bounds[1]
    block = first + step
    rows = q_ref.shape[0]
    kind = kinds[step]

    @pl.when(step == 0)
    def _():
        m_sc[...] = jnp.full(m_sc.shape, NEGATIVE, jnp.float32)
        l_sc[...] = jnp.zeros(l_sc.shape, jnp.float32)
        acc_sc[...] = jnp.zeros(acc_sc.shape, jnp.float32)

    def absorb(masked):
        keys = kv_ref[0]
        values = jnp.concatenate([kv_ref[1], jnp.ones((rows, HEAD_DIM), jnp.bfloat16)], axis=1)
        if masked:
            query_places = own * rows + lax.broadcasted_iota(jnp.int32, (rows, rows), 0)
            key_places = block * rows + lax.broadcasted_iota(jnp.int32, (rows, rows), 1)
            allowed = (qseg_ref[...] == kseg_ref[...]) & (key_places <= query_places)
        for h in range(heads):
            query = q_ref[:, h * HEAD_DIM:(h + 1) * HEAD_DIM]
            scores = lax.dot_general(
                query, keys, (((1,), (1,)), ((), ())), preferred_element_type=jnp.float32
            ) * HEAD_DIM ** (-0.5)
            if masked:
                scores = jnp.where(allowed, scores, NEGATIVE)
            highest = jnp.max(scores, axis=1, keepdims=True)
            raised = jnp.exp(scores - highest)
            if masked:
                raised = jnp.where(allowed, raised, 0.0)
            both = jnp.dot(raised.astype(jnp.bfloat16), values, preferred_element_type=jnp.float32)
            numerator = both[:, :HEAD_DIM]
            denominator = both[:, HEAD_DIM:]
            previous = m_sc[h]
            summit = jnp.maximum(previous, highest)
            retain = jnp.exp(previous - summit)
            admit = jnp.exp(highest - summit)
            acc_sc[h] = acc_sc[h] * retain + numerator * admit
            l_sc[h] = l_sc[h] * retain + denominator * admit
            m_sc[h] = summit

    @pl.when(kind == 1)
    def _():
        absorb(False)

    @pl.when(kind == 2)
    def _():
        absorb(True)

    @pl.when(step == pl.num_programs(0) - 1)
    def _():
        for h in range(heads):
            o_ref[:, h * HEAD_DIM:(h + 1) * HEAD_DIM] = (acc_sc[h] / l_sc[h]).astype(o_ref.dtype)


def flash(bounds, kinds, queries, gathered, key_segments, query_segments, steps):
    rows, width = queries.shape
    heads = width // HEAD_DIM

    def kv_map(step, b, k):
        return (jnp.minimum(b[0] + step, b[1]) - b[1] + steps - 1, 0, 0, 0)

    def kseg_map(step, b, k):
        return (0, jnp.minimum(b[0] + step, b[1]))

    grid_spec = pltpu.PrefetchScalarGridSpec(
        num_scalar_prefetch=2,
        grid=(steps,),
        in_specs=[
            pl.BlockSpec((rows, width), lambda step, b, k: (0, 0)),
            pl.BlockSpec((None, 2, rows, HEAD_DIM), kv_map),
            pl.BlockSpec((1, rows), kseg_map),
            pl.BlockSpec((rows, 1), lambda step, b, k: (0, 0)),
        ],
        out_specs=pl.BlockSpec((rows, width), lambda step, b, k: (0, 0)),
        scratch_shapes=[
            pltpu.VMEM((heads, rows, HEAD_DIM), jnp.float32),
            pltpu.VMEM((heads, rows, HEAD_DIM), jnp.float32),
            pltpu.VMEM((heads, rows, HEAD_DIM), jnp.float32),
        ],
    )
    return pl.pallas_call(
        functools.partial(flash_kernel, heads=heads),
        grid_spec=grid_spec,
        out_shape=jax.ShapeDtypeStruct((rows, width), jnp.bfloat16),
    )(bounds, kinds, queries, gathered, key_segments, query_segments)


def steps_needed(shard_rows, ctx_count):
    return min(ctx_count, -(-(MOST - 1) // shard_rows) + 1)


def earlier_blocks(packed, axis, span):
    count = lax.axis_size(axis)
    place = lax.axis_index(axis)
    reach = span // 2
    chain = [packed]
    for k in range(1, reach + 1):
        pairs = [(i, i + 2 * k) for i in range(count - 2 * k)]
        chain.append(lax.ppermute(packed, axis, pairs))
    own = jnp.stack(chain)
    sibling = lax.ppermute(own, axis, [(i, i ^ 1) for i in range(count)])
    backward = sibling[::-1]
    odd = jnp.where(place % 2 == 0, backward[0:reach], backward[1:reach + 1])
    even = own[::-1]
    window = jnp.stack([even[:reach], odd], axis=1).reshape((2 * reach,) + packed.shape)
    return jnp.concatenate([window, own[:1]], 0)


def on_device(tokens, doc_lengths, norm_gain, w_query, w_key, w_value, w_out):
    shard_rows = tokens.shape[0]
    ctx_count = lax.axis_size("ctx")
    ctx_place = lax.axis_index("ctx")
    starts = doc_starts(doc_lengths)
    local_places = jnp.arange(shard_rows, dtype=jnp.int32)
    positions = ctx_place * shard_rows + local_places
    segment, doc_first = seg_info(positions, starts)
    every_place = jnp.arange(shard_rows * ctx_count, dtype=jnp.int32)
    every_segment, unused_first = seg_info(every_place, starts)
    normed = normalize(tokens, norm_gain)
    offsets = positions - doc_first
    queries = project(normed, w_query, offsets).reshape(shard_rows, -1)
    keys = project(normed, w_key, offsets).reshape(shard_rows, -1)
    values = jnp.dot(normed, w_value, preferred_element_type=jnp.float32).astype(jnp.bfloat16)
    packed = jnp.stack([keys, values])
    gathered = earlier_blocks(packed, "ctx", steps_needed(shard_rows, ctx_count))
    bounds = jnp.stack([doc_first[0] // shard_rows, ctx_place]).astype(jnp.int32)
    steps = steps_needed(shard_rows, ctx_count)
    visited = bounds[0] + jnp.arange(steps, dtype=jnp.int32)
    head_segment = every_segment[jnp.minimum(visited, ctx_place) * shard_rows]
    whole = (visited < ctx_place) & (head_segment == segment[shard_rows - 1])
    kinds = jnp.where(visited > ctx_place, 0, jnp.where(whole, 1, 2)).astype(jnp.int32)
    attended = flash(
        bounds,
        kinds,
        queries,
        gathered,
        every_segment.reshape(1, -1).astype(jnp.int32),
        segment.reshape(-1, 1).astype(jnp.int32),
        steps,
    )
    partial_value = jnp.dot(attended, w_out, preferred_element_type=jnp.float32)
    return scatter_sum(partial_value.astype(jnp.bfloat16), "tp")


def scatter_sum(partial_value, axis):
    count = lax.axis_size(axis)
    place = lax.axis_index(axis)
    chunks = partial_value.reshape(partial_value.shape[0], count, -1)
    rightward = [(i, (i + 1) % count) for i in range(count)]
    leftward = [(i, (i - 1) % count) for i in range(count)]

    def pick(index):
        return lax.dynamic_index_in_dim(chunks, index % count, axis=1, keepdims=False).astype(
            jnp.float32
        )

    reach_right = count // 2
    reach_left = count - 1 - reach_right
    from_left = pick(place + reach_right)
    from_right = pick(place - reach_left)
    for hop in range(1, reach_right + 1):
        from_left = lax.ppermute(from_left.astype(jnp.bfloat16), axis, rightward).astype(jnp.float32)
        if hop <= reach_left:
            from_right = lax.ppermute(from_right.astype(jnp.bfloat16), axis, leftward).astype(
                jnp.float32
            )
        if hop < reach_right:
            from_left = from_left + pick(place + reach_right - hop)
        if hop < reach_left:
            from_right = from_right + pick(place - reach_left + hop)
    return (from_left + from_right + pick(place)).astype(jnp.bfloat16)


def solution(mesh):
    placed = (P("ctx", None), P(), P(), P(None, "tp"), P(None, "tp"), P(None, "tp"), P("tp", None))
    return jax.shard_map(
        on_device, mesh=mesh, in_specs=placed, out_specs=P("ctx", "tp"), check_vma=False
    )
```

```python
import functools

import jax
import jax.numpy as jnp
from jax import lax
from jax.experimental import pallas as pl
from jax.experimental.pallas import tpu as pltpu
from jax.sharding import PartitionSpec as P

HEAD_DIM = 128
MOST = 4096


NEGATIVE = -1e30
ROPE_BASE = 500000.0
EPSILON = 1e-05


def doc_starts(doc_lengths):
    ends = jnp.cumsum(doc_lengths)
    return ends - doc_lengths


def seg_info(positions, starts):
    inside = starts[None, :] <= positions[:, None]
    segment = jnp.sum(inside.astype(jnp.int32), axis=1) - 1
    doc_first = jnp.max(jnp.where(inside, starts[None, :], 0), axis=1)
    return (segment, doc_first)


def rotate(lifted, offsets):
    halfway = lifted.shape[-1] // 2
    fraction = jnp.arange(halfway, dtype=jnp.float32) * (2.0 / lifted.shape[-1])
    inverse = jnp.exp(-jnp.log(jnp.float32(ROPE_BASE)) * fraction)
    angles = offsets.astype(jnp.float32)[:, None] * inverse[None, :]
    cosine = jnp.cos(angles)[:, None, :]
    sine_table = jnp.sin(angles)[:, None, :]
    leading = lifted[..., :halfway]
    trailing = lifted[..., halfway:]
    return jnp.concatenate(
        [leading * cosine - trailing * sine_table, trailing * cosine + leading * sine_table],
        axis=-1,
    )


def normalize(tokens, norm_gain):
    widened = tokens.astype(jnp.float32)
    square = jnp.mean(widened * widened, axis=-1, keepdims=True)
    return (widened * lax.rsqrt(square + EPSILON) * norm_gain.astype(jnp.float32)).astype(
        jnp.bfloat16
    )


def project(normed, weight, offsets):
    head_count = weight.shape[1] // HEAD_DIM
    lifted = jnp.dot(normed, weight, preferred_element_type=jnp.float32)
    lifted = lifted.reshape(normed.shape[0], head_count, HEAD_DIM)
    return rotate(lifted, offsets).astype(jnp.bfloat16)


def flash_kernel(bounds, kinds, q_ref, kv_ref, kseg_ref, qseg_ref, o_ref, m_sc, l_sc, acc_sc, *, heads):
    step = pl.program_id(0)
    first = bounds[0]
    own = bounds[1]
    block = first + step
    rows = q_ref.shape[0]
    kind = kinds[step]

    @pl.when(step == 0)
    def _():
        m_sc[...] = jnp.full(m_sc.shape, NEGATIVE, jnp.float32)
        l_sc[...] = jnp.zeros(l_sc.shape, jnp.float32)
        acc_sc[...] = jnp.zeros(acc_sc.shape, jnp.float32)

    def absorb(masked):
        keys = kv_ref[0]
        values = jnp.concatenate([kv_ref[1], jnp.ones((rows, HEAD_DIM), jnp.bfloat16)], axis=1)
        if masked:
            query_places = own * rows + lax.broadcasted_iota(jnp.int32, (rows, rows), 0)
            key_places = block * rows + lax.broadcasted_iota(jnp.int32, (rows, rows), 1)
            allowed = (qseg_ref[...] == kseg_ref[...]) & (key_places <= query_places)
        for h in range(heads):
            query = q_ref[:, h * HEAD_DIM:(h + 1) * HEAD_DIM]
            scores = lax.dot_general(
                query, keys, (((1,), (1,)), ((), ())), preferred_element_type=jnp.float32
            ) * HEAD_DIM ** (-0.5)
            if masked:
                scores = jnp.where(allowed, scores, NEGATIVE)
            highest = jnp.max(scores, axis=1, keepdims=True)
            raised = jnp.exp(scores - highest)
            if masked:
                raised = jnp.where(allowed, raised, 0.0)
            both = jnp.dot(raised.astype(jnp.bfloat16), values, preferred_element_type=jnp.float32)
            numerator = both[:, :HEAD_DIM]
            denominator = both[:, HEAD_DIM:]
            previous = m_sc[h]
            summit = jnp.maximum(previous, highest)
            retain = jnp.exp(previous - summit)
            admit = jnp.exp(highest - summit)
            acc_sc[h] = acc_sc[h] * retain + numerator * admit
            l_sc[h] = l_sc[h] * retain + denominator * admit
            m_sc[h] = summit

    @pl.when(kind == 1)
    def _():
        absorb(False)

    @pl.when(kind == 2)
    def _():
        absorb(True)

    @pl.when(step == pl.num_programs(0) - 1)
    def _():
        for h in range(heads):
            o_ref[:, h * HEAD_DIM:(h + 1) * HEAD_DIM] = (acc_sc[h] / l_sc[h]).astype(o_ref.dtype)


def flash(bounds, kinds, queries, gathered, key_segments, query_segments, steps):
    rows, width = queries.shape
    heads = width // HEAD_DIM

    def kv_map(step, b, k):
        return (jnp.minimum(b[0] + step, b[1]) - b[1] + steps - 1, 0, 0, 0)

    def kseg_map(step, b, k):
        return (0, jnp.minimum(b[0] + step, b[1]))

    grid_spec = pltpu.PrefetchScalarGridSpec(
        num_scalar_prefetch=2,
        grid=(steps,),
        in_specs=[
            pl.BlockSpec((rows, width), lambda step, b, k: (0, 0)),
            pl.BlockSpec((None, 2, rows, HEAD_DIM), kv_map),
            pl.BlockSpec((1, rows), kseg_map),
            pl.BlockSpec((rows, 1), lambda step, b, k: (0, 0)),
        ],
        out_specs=pl.BlockSpec((rows, width), lambda step, b, k: (0, 0)),
        scratch_shapes=[
            pltpu.VMEM((heads, rows, HEAD_DIM), jnp.float32),
            pltpu.VMEM((heads, rows, HEAD_DIM), jnp.float32),
            pltpu.VMEM((heads, rows, HEAD_DIM), jnp.float32),
        ],
    )
    return pl.pallas_call(
        functools.partial(flash_kernel, heads=heads),
        grid_spec=grid_spec,
        out_shape=jax.ShapeDtypeStruct((rows, width), jnp.bfloat16),
    )(bounds, kinds, queries, gathered, key_segments, query_segments)


def steps_needed(shard_rows, ctx_count):
    return min(ctx_count, -(-(MOST - 1) // shard_rows) + 1)


def earlier_blocks(packed, axis, span):
    count = lax.axis_size(axis)
    place = lax.axis_index(axis)
    reach = span // 2
    chain = [packed]
    for k in range(1, reach + 1):
        pairs = [(i, i + 2 * k) for i in range(count - 2 * k)]
        chain.append(lax.ppermute(packed, axis, pairs))
    sibling = lax.ppermute(tuple(chain), axis, [(i, i ^ 1) for i in range(count)])
    even_core = place % 2 == 0
    parts = []
    for m in range(reach):
        parts.append(chain[reach - m])
        parts.append(jnp.where(even_core, sibling[reach - m], sibling[reach - 1 - m]))
    parts.append(packed)
    return jnp.stack(parts)


def on_device(tokens, doc_lengths, norm_gain, w_query, w_key, w_value, w_out):
    shard_rows = tokens.shape[0]
    ctx_count = lax.axis_size("ctx")
    ctx_place = lax.axis_index("ctx")
    starts = doc_starts(doc_lengths)
    local_places = jnp.arange(shard_rows, dtype=jnp.int32)
    positions = ctx_place * shard_rows + local_places
    segment, doc_first = seg_info(positions, starts)
    every_place = jnp.arange(shard_rows * ctx_count, dtype=jnp.int32)
    every_segment, unused_first = seg_info(every_place, starts)
    normed = normalize(tokens, norm_gain)
    offsets = positions - doc_first
    queries = project(normed, w_query, offsets).reshape(shard_rows, -1)
    keys = project(normed, w_key, offsets).reshape(shard_rows, -1)
    values = jnp.dot(normed, w_value, preferred_element_type=jnp.float32).astype(jnp.bfloat16)
    packed = jnp.stack([keys, values])
    gathered = earlier_blocks(packed, "ctx", steps_needed(shard_rows, ctx_count))
    bounds = jnp.stack([doc_first[0] // shard_rows, ctx_place]).astype(jnp.int32)
    steps = steps_needed(shard_rows, ctx_count)
    visited = bounds[0] + jnp.arange(steps, dtype=jnp.int32)
    head_segment = every_segment[jnp.minimum(visited, ctx_place) * shard_rows]
    whole = (visited < ctx_place) & (head_segment == segment[shard_rows - 1])
    kinds = jnp.where(visited > ctx_place, 0, jnp.where(whole, 1, 2)).astype(jnp.int32)
    attended = flash(
        bounds,
        kinds,
        queries,
        gathered,
        every_segment.reshape(1, -1).astype(jnp.int32),
        segment.reshape(-1, 1).astype(jnp.int32),
        steps,
    )
    partial_value = jnp.dot(attended, w_out, preferred_element_type=jnp.float32)
    return scatter_sum(partial_value.astype(jnp.bfloat16), "tp")


def scatter_sum(partial_value, axis):
    count = lax.axis_size(axis)
    place = lax.axis_index(axis)
    chunks = partial_value.reshape(partial_value.shape[0], count, -1)
    rightward = [(i, (i + 1) % count) for i in range(count)]
    leftward = [(i, (i - 1) % count) for i in range(count)]

    def pick(index):
        return lax.dynamic_index_in_dim(chunks, index % count, axis=1, keepdims=False).astype(
            jnp.float32
        )

    reach_right = count // 2
    reach_left = count - 1 - reach_right
    from_left = pick(place + reach_right)
    from_right = pick(place - reach_left)
    for hop in range(1, reach_right + 1):
        from_left = lax.ppermute(from_left.astype(jnp.bfloat16), axis, rightward).astype(jnp.float32)
        if hop <= reach_left:
            from_right = lax.ppermute(from_right.astype(jnp.bfloat16), axis, leftward).astype(
                jnp.float32
            )
        if hop < reach_right:
            from_left = from_left + pick(place + reach_right - hop)
        if hop < reach_left:
            from_right = from_right + pick(place - reach_left + hop)
    return (from_left + from_right + pick(place)).astype(jnp.bfloat16)


def solution(mesh):
    placed = (P("ctx", None), P(), P(), P(None, "tp"), P(None, "tp"), P(None, "tp"), P("tp", None))
    return jax.shard_map(
        on_device, mesh=mesh, in_specs=placed, out_specs=P("ctx", "tp"), check_vma=False
    )
```

```python
import functools

import jax
import jax.numpy as jnp
from jax import lax
from jax.experimental import pallas as pl
from jax.experimental.pallas import tpu as pltpu
from jax.sharding import PartitionSpec as P

HEAD_DIM = 128
MOST = 4096


NEGATIVE = -1e30
ROPE_BASE = 500000.0
EPSILON = 1e-05


def doc_starts(doc_lengths):
    ends = jnp.cumsum(doc_lengths)
    return ends - doc_lengths


def seg_info(positions, starts):
    inside = starts[None, :] <= positions[:, None]
    segment = jnp.sum(inside.astype(jnp.int32), axis=1) - 1
    doc_first = jnp.max(jnp.where(inside, starts[None, :], 0), axis=1)
    return (segment, doc_first)


def rotate(lifted, offsets):
    halfway = lifted.shape[-1] // 2
    fraction = jnp.arange(halfway, dtype=jnp.float32) * (2.0 / lifted.shape[-1])
    inverse = jnp.exp(-jnp.log(jnp.float32(ROPE_BASE)) * fraction)
    angles = offsets.astype(jnp.float32)[:, None] * inverse[None, :]
    cosine = jnp.cos(angles)[:, None, :]
    sine_table = jnp.sin(angles)[:, None, :]
    leading = lifted[..., :halfway]
    trailing = lifted[..., halfway:]
    return jnp.concatenate(
        [leading * cosine - trailing * sine_table, trailing * cosine + leading * sine_table],
        axis=-1,
    )


def normalize(tokens, norm_gain):
    widened = tokens.astype(jnp.float32)
    square = jnp.mean(widened * widened, axis=-1, keepdims=True)
    return (widened * lax.rsqrt(square + EPSILON) * norm_gain.astype(jnp.float32)).astype(
        jnp.bfloat16
    )


def project(normed, weight, offsets):
    head_count = weight.shape[1] // HEAD_DIM
    lifted = jnp.dot(normed, weight, preferred_element_type=jnp.float32)
    lifted = lifted.reshape(normed.shape[0], head_count, HEAD_DIM)
    return rotate(lifted, offsets).astype(jnp.bfloat16)


def flash_kernel(bounds, kinds, q_ref, kv_ref, kseg_ref, qseg_ref, o_ref, m_sc, l_sc, acc_sc, *, heads):
    step = pl.program_id(0)
    first = bounds[0]
    own = bounds[1]
    block = first + step
    rows = q_ref.shape[0]
    kind = kinds[step]

    @pl.when(step == 0)
    def _():
        m_sc[...] = jnp.full(m_sc.shape, NEGATIVE, jnp.float32)
        l_sc[...] = jnp.zeros(l_sc.shape, jnp.float32)
        acc_sc[...] = jnp.zeros(acc_sc.shape, jnp.float32)

    def absorb(masked):
        keys = kv_ref[0]
        values = jnp.concatenate([kv_ref[1], jnp.ones((rows, HEAD_DIM), jnp.bfloat16)], axis=1)
        if masked:
            query_places = own * rows + lax.broadcasted_iota(jnp.int32, (rows, rows), 0)
            key_places = block * rows + lax.broadcasted_iota(jnp.int32, (rows, rows), 1)
            allowed = (qseg_ref[...] == kseg_ref[...]) & (key_places <= query_places)
        for h in range(heads):
            query = q_ref[:, h * HEAD_DIM:(h + 1) * HEAD_DIM]
            scores = lax.dot_general(
                query, keys, (((1,), (1,)), ((), ())), preferred_element_type=jnp.float32
            ) * HEAD_DIM ** (-0.5)
            if masked:
                scores = jnp.where(allowed, scores, NEGATIVE)
            highest = jnp.max(scores, axis=1, keepdims=True)
            raised = jnp.exp(scores - highest)
            if masked:
                raised = jnp.where(allowed, raised, 0.0)
            both = jnp.dot(raised.astype(jnp.bfloat16), values, preferred_element_type=jnp.float32)
            numerator = both[:, :HEAD_DIM]
            denominator = both[:, HEAD_DIM:]
            previous = m_sc[h]
            summit = jnp.maximum(previous, highest)
            retain = jnp.exp(previous - summit)
            admit = jnp.exp(highest - summit)
            acc_sc[h] = acc_sc[h] * retain + numerator * admit
            l_sc[h] = l_sc[h] * retain + denominator * admit
            m_sc[h] = summit

    @pl.when(kind == 1)
    def _():
        absorb(False)

    @pl.when(kind == 2)
    def _():
        absorb(True)

    @pl.when(step == pl.num_programs(0) - 1)
    def _():
        for h in range(heads):
            o_ref[:, h * HEAD_DIM:(h + 1) * HEAD_DIM] = (acc_sc[h] / l_sc[h]).astype(o_ref.dtype)


def flash(bounds, kinds, queries, gathered, key_segments, query_segments, steps):
    rows, width = queries.shape
    heads = width // HEAD_DIM

    def kv_map(step, b, k):
        return (jnp.minimum(b[0] + step, b[1]) - b[1] + steps - 1, 0, 0, 0)

    def kseg_map(step, b, k):
        return (0, jnp.minimum(b[0] + step, b[1]))

    grid_spec = pltpu.PrefetchScalarGridSpec(
        num_scalar_prefetch=2,
        grid=(steps,),
        in_specs=[
            pl.BlockSpec((rows, width), lambda step, b, k: (0, 0)),
            pl.BlockSpec((None, 2, rows, HEAD_DIM), kv_map),
            pl.BlockSpec((1, rows), kseg_map),
            pl.BlockSpec((rows, 1), lambda step, b, k: (0, 0)),
        ],
        out_specs=pl.BlockSpec((rows, width), lambda step, b, k: (0, 0)),
        scratch_shapes=[
            pltpu.VMEM((heads, rows, HEAD_DIM), jnp.float32),
            pltpu.VMEM((heads, rows, HEAD_DIM), jnp.float32),
            pltpu.VMEM((heads, rows, HEAD_DIM), jnp.float32),
        ],
    )
    return pl.pallas_call(
        functools.partial(flash_kernel, heads=heads),
        grid_spec=grid_spec,
        out_shape=jax.ShapeDtypeStruct((rows, width), jnp.bfloat16),
    )(bounds, kinds, queries, gathered, key_segments, query_segments)


def steps_needed(shard_rows, ctx_count):
    return min(ctx_count, -(-(MOST - 1) // shard_rows) + 1)


def earlier_blocks(packed, axis, span):
    count = lax.axis_size(axis)
    place = lax.axis_index(axis)
    reach = span // 2
    chain = [packed]
    for k in range(1, reach + 1):
        pairs = [(i, i + 2 * k) for i in range(count - 2 * k)]
        chain.append(lax.ppermute(packed, axis, pairs))
    sibling = lax.ppermute(tuple(chain), axis, [(i, i ^ 1) for i in range(count)])
    even_core = place % 2 == 0
    parts = []
    for m in range(reach):
        parts.append(chain[reach - m])
        parts.append(jnp.where(even_core, sibling[reach - m], sibling[reach - 1 - m]))
    parts.append(packed)
    return jnp.stack(parts)


def on_device(tokens, doc_lengths, norm_gain, w_query, w_key, w_value, w_out):
    shard_rows = tokens.shape[0]
    ctx_count = lax.axis_size("ctx")
    ctx_place = lax.axis_index("ctx")
    starts = doc_starts(doc_lengths)
    local_places = jnp.arange(shard_rows, dtype=jnp.int32)
    positions = ctx_place * shard_rows + local_places
    segment, doc_first = seg_info(positions, starts)
    every_place = jnp.arange(shard_rows * ctx_count, dtype=jnp.int32)
    every_segment, unused_first = seg_info(every_place, starts)
    normed = normalize(tokens, norm_gain)
    offsets = positions - doc_first
    queries = project(normed, w_query, offsets).reshape(shard_rows, -1)
    keys = project(normed, w_key, offsets).reshape(shard_rows, -1)
    values = jnp.dot(normed, w_value, preferred_element_type=jnp.float32).astype(jnp.bfloat16)
    packed = jnp.stack([keys, values])
    gathered = earlier_blocks(packed, "ctx", steps_needed(shard_rows, ctx_count))
    bounds = jnp.stack([doc_first[0] // shard_rows, ctx_place]).astype(jnp.int32)
    steps = steps_needed(shard_rows, ctx_count)
    visited = bounds[0] + jnp.arange(steps, dtype=jnp.int32)
    head_segment = every_segment[jnp.minimum(visited, ctx_place) * shard_rows]
    whole = (visited < ctx_place) & (head_segment == segment[shard_rows - 1])
    kinds = jnp.where(visited > ctx_place, 0, jnp.where(whole, 1, 2)).astype(jnp.int32)
    attended = flash(
        bounds,
        kinds,
        queries,
        gathered,
        every_segment.reshape(1, -1).astype(jnp.int32),
        segment.reshape(-1, 1).astype(jnp.int32),
        steps,
    )
    return scatter_sum(attended, w_out, "tp")


def scatter_sum(attended, w_out, axis):
    count = lax.axis_size(axis)
    place = lax.axis_index(axis)
    width = w_out.shape[1] // count
    rightward = [(i, (i + 1) % count) for i in range(count)]
    leftward = [(i, (i - 1) % count) for i in range(count)]

    def pick(index):
        columns = lax.dynamic_slice_in_dim(w_out, (index % count) * width, width, axis=1)
        partial_value = jnp.dot(attended, columns, preferred_element_type=jnp.float32)
        return partial_value.astype(jnp.bfloat16).astype(jnp.float32)

    reach_right = count // 2
    reach_left = count - 1 - reach_right
    from_left = pick(place + reach_right)
    from_right = pick(place - reach_left)
    for hop in range(1, reach_right + 1):
        from_left = lax.ppermute(from_left.astype(jnp.bfloat16), axis, rightward).astype(jnp.float32)
        if hop <= reach_left:
            from_right = lax.ppermute(from_right.astype(jnp.bfloat16), axis, leftward).astype(
                jnp.float32
            )
        if hop < reach_right:
            from_left = from_left + pick(place + reach_right - hop)
        if hop < reach_left:
            from_right = from_right + pick(place - reach_left + hop)
    return (from_left + from_right + pick(place)).astype(jnp.bfloat16)


def solution(mesh):
    placed = (P("ctx", None), P(), P(), P(None, "tp"), P(None, "tp"), P(None, "tp"), P("tp", None))
    return jax.shard_map(
        on_device, mesh=mesh, in_specs=placed, out_specs=P("ctx", "tp"), check_vma=False
    )
```

```python
import functools

import jax
import jax.numpy as jnp
from jax import lax
from jax.experimental import pallas as pl
from jax.experimental.pallas import tpu as pltpu
from jax.sharding import PartitionSpec as P

HEAD_DIM = 128
MOST = 4096


NEGATIVE = -1e30
ROPE_BASE = 500000.0
EPSILON = 1e-05


def doc_starts(doc_lengths):
    ends = jnp.cumsum(doc_lengths)
    return ends - doc_lengths


def seg_info(positions, starts):
    inside = starts[None, :] <= positions[:, None]
    segment = jnp.sum(inside.astype(jnp.int32), axis=1) - 1
    doc_first = jnp.max(jnp.where(inside, starts[None, :], 0), axis=1)
    return (segment, doc_first)


def rotate(lifted, offsets):
    halfway = lifted.shape[-1] // 2
    fraction = jnp.arange(halfway, dtype=jnp.float32) * (2.0 / lifted.shape[-1])
    inverse = jnp.exp(-jnp.log(jnp.float32(ROPE_BASE)) * fraction)
    angles = offsets.astype(jnp.float32)[:, None] * inverse[None, :]
    cosine = jnp.cos(angles)[:, None, :]
    sine_table = jnp.sin(angles)[:, None, :]
    leading = lifted[..., :halfway]
    trailing = lifted[..., halfway:]
    return jnp.concatenate(
        [leading * cosine - trailing * sine_table, trailing * cosine + leading * sine_table],
        axis=-1,
    )


def normalize(tokens, norm_gain):
    widened = tokens.astype(jnp.float32)
    square = jnp.mean(widened * widened, axis=-1, keepdims=True)
    return (widened * lax.rsqrt(square + EPSILON) * norm_gain.astype(jnp.float32)).astype(
        jnp.bfloat16
    )


def project(normed, weight, offsets):
    head_count = weight.shape[1] // HEAD_DIM
    lifted = jnp.dot(normed, weight, preferred_element_type=jnp.float32)
    lifted = lifted.reshape(normed.shape[0], head_count, HEAD_DIM)
    return rotate(lifted, offsets).astype(jnp.bfloat16)


def flash_kernel(bounds, kinds, picks, q_ref, kseg_ref, qseg_ref, *rest, heads):
    o_ref, kv_ref, m_sc, l_sc, acc_sc = rest[-5:]
    part_refs = rest[:-5]
    step = pl.program_id(0)
    first = bounds[0]
    own = bounds[1]
    block = first + step
    rows = q_ref.shape[0]
    kind = kinds[step]

    @pl.when(step == 0)
    def _():
        m_sc[...] = jnp.full(m_sc.shape, NEGATIVE, jnp.float32)
        l_sc[...] = jnp.zeros(l_sc.shape, jnp.float32)
        acc_sc[...] = jnp.zeros(acc_sc.shape, jnp.float32)

    for index, part in enumerate(part_refs):

        @pl.when((kind > 0) & (picks[step] == index))
        def _():
            kv_ref[...] = part[...]

    def absorb(masked):
        keys = kv_ref[0]
        values = jnp.concatenate([kv_ref[1], jnp.ones((rows, HEAD_DIM), jnp.bfloat16)], axis=1)
        if masked:
            query_places = own * rows + lax.broadcasted_iota(jnp.int32, (rows, rows), 0)
            key_places = block * rows + lax.broadcasted_iota(jnp.int32, (rows, rows), 1)
            allowed = (qseg_ref[...] == kseg_ref[...]) & (key_places <= query_places)
        for h in range(heads):
            query = q_ref[:, h * HEAD_DIM:(h + 1) * HEAD_DIM]
            scores = lax.dot_general(
                query, keys, (((1,), (1,)), ((), ())), preferred_element_type=jnp.float32
            ) * HEAD_DIM ** (-0.5)
            if masked:
                scores = jnp.where(allowed, scores, NEGATIVE)
            highest = jnp.max(scores, axis=1, keepdims=True)
            raised = jnp.exp(scores - highest)
            if masked:
                raised = jnp.where(allowed, raised, 0.0)
            both = jnp.dot(raised.astype(jnp.bfloat16), values, preferred_element_type=jnp.float32)
            numerator = both[:, :HEAD_DIM]
            denominator = both[:, HEAD_DIM:]
            previous = m_sc[h]
            summit = jnp.maximum(previous, highest)
            retain = jnp.exp(previous - summit)
            admit = jnp.exp(highest - summit)
            acc_sc[h] = acc_sc[h] * retain + numerator * admit
            l_sc[h] = l_sc[h] * retain + denominator * admit
            m_sc[h] = summit

    @pl.when(kind == 1)
    def _():
        absorb(False)

    @pl.when(kind == 2)
    def _():
        absorb(True)

    @pl.when(step == pl.num_programs(0) - 1)
    def _():
        for h in range(heads):
            o_ref[:, h * HEAD_DIM:(h + 1) * HEAD_DIM] = (acc_sc[h] / l_sc[h]).astype(o_ref.dtype)


def flash(bounds, kinds, picks, queries, parts, key_segments, query_segments, steps):
    rows, width = queries.shape
    heads = width // HEAD_DIM

    def kseg_map(step, b, k, p):
        return (0, jnp.minimum(b[0] + step, b[1]))

    def whole(step, b, k, p):
        return (0, 0, 0)

    grid_spec = pltpu.PrefetchScalarGridSpec(
        num_scalar_prefetch=3,
        grid=(steps,),
        in_specs=[
            pl.BlockSpec((rows, width), lambda step, b, k, p: (0, 0)),
            pl.BlockSpec((1, rows), kseg_map),
            pl.BlockSpec((rows, 1), lambda step, b, k, p: (0, 0)),
        ]
        + [pl.BlockSpec(part.shape, whole) for part in parts],
        out_specs=pl.BlockSpec((rows, width), lambda step, b, k, p: (0, 0)),
        scratch_shapes=[
            pltpu.VMEM(parts[0].shape, parts[0].dtype),
            pltpu.VMEM((heads, rows, HEAD_DIM), jnp.float32),
            pltpu.VMEM((heads, rows, HEAD_DIM), jnp.float32),
            pltpu.VMEM((heads, rows, HEAD_DIM), jnp.float32),
        ],
    )
    return pl.pallas_call(
        functools.partial(flash_kernel, heads=heads),
        grid_spec=grid_spec,
        out_shape=jax.ShapeDtypeStruct((rows, width), jnp.bfloat16),
    )(bounds, kinds, picks, queries, key_segments, query_segments, *parts)


def steps_needed(shard_rows, ctx_count):
    return min(ctx_count, -(-(MOST - 1) // shard_rows) + 1)


def earlier_blocks(packed, axis, span):
    count = lax.axis_size(axis)
    reach = span // 2
    chain = [packed]
    for k in range(1, reach + 1):
        pairs = [(i, i + 2 * k) for i in range(count - 2 * k)]
        chain.append(lax.ppermute(packed, axis, pairs))
    sibling = lax.ppermute(tuple(chain), axis, [(i, i ^ 1) for i in range(count)])
    return chain + list(sibling)


def part_of(offset, place, reach):
    sibling_index = reach + 1 + (offset + 1 - 2 * (place % 2)) // 2
    return jnp.where(offset % 2 == 0, offset // 2, sibling_index)


def on_device(tokens, doc_lengths, norm_gain, w_query, w_key, w_value, w_out):
    shard_rows = tokens.shape[0]
    ctx_count = lax.axis_size("ctx")
    ctx_place = lax.axis_index("ctx")
    starts = doc_starts(doc_lengths)
    local_places = jnp.arange(shard_rows, dtype=jnp.int32)
    positions = ctx_place * shard_rows + local_places
    segment, doc_first = seg_info(positions, starts)
    every_place = jnp.arange(shard_rows * ctx_count, dtype=jnp.int32)
    every_segment, unused_first = seg_info(every_place, starts)
    normed = normalize(tokens, norm_gain)
    offsets = positions - doc_first
    queries = project(normed, w_query, offsets).reshape(shard_rows, -1)
    keys = project(normed, w_key, offsets).reshape(shard_rows, -1)
    values = jnp.dot(normed, w_value, preferred_element_type=jnp.float32).astype(jnp.bfloat16)
    packed = jnp.stack([keys, values])
    gathered = earlier_blocks(packed, "ctx", steps_needed(shard_rows, ctx_count))
    bounds = jnp.stack([doc_first[0] // shard_rows, ctx_place]).astype(jnp.int32)
    steps = steps_needed(shard_rows, ctx_count)
    visited = bounds[0] + jnp.arange(steps, dtype=jnp.int32)
    head_segment = every_segment[jnp.minimum(visited, ctx_place) * shard_rows]
    whole = (visited < ctx_place) & (head_segment == segment[shard_rows - 1])
    kinds = jnp.where(visited > ctx_place, 0, jnp.where(whole, 1, 2)).astype(jnp.int32)
    offsets_back = ctx_place - jnp.minimum(visited, ctx_place)
    picks = part_of(offsets_back, ctx_place, steps // 2).astype(jnp.int32)
    attended = flash(
        bounds,
        kinds,
        picks,
        queries,
        gathered,
        every_segment.reshape(1, -1).astype(jnp.int32),
        segment.reshape(-1, 1).astype(jnp.int32),
        steps,
    )
    return scatter_sum(attended, w_out, "tp")


def scatter_sum(attended, w_out, axis):
    count = lax.axis_size(axis)
    place = lax.axis_index(axis)
    width = w_out.shape[1] // count
    rightward = [(i, (i + 1) % count) for i in range(count)]
    leftward = [(i, (i - 1) % count) for i in range(count)]

    def pick(index):
        columns = lax.dynamic_slice_in_dim(w_out, (index % count) * width, width, axis=1)
        partial_value = jnp.dot(attended, columns, preferred_element_type=jnp.float32)
        return partial_value.astype(jnp.bfloat16).astype(jnp.float32)

    reach_right = count // 2
    reach_left = count - 1 - reach_right
    from_left = pick(place + reach_right)
    from_right = pick(place - reach_left)
    for hop in range(1, reach_right + 1):
        from_left = lax.ppermute(from_left.astype(jnp.bfloat16), axis, rightward).astype(jnp.float32)
        if hop <= reach_left:
            from_right = lax.ppermute(from_right.astype(jnp.bfloat16), axis, leftward).astype(
                jnp.float32
            )
        if hop < reach_right:
            from_left = from_left + pick(place + reach_right - hop)
        if hop < reach_left:
            from_right = from_right + pick(place - reach_left + hop)
    return (from_left + from_right + pick(place)).astype(jnp.bfloat16)


def solution(mesh):
    placed = (P("ctx", None), P(), P(), P(None, "tp"), P(None, "tp"), P(None, "tp"), P("tp", None))
    return jax.shard_map(
        on_device, mesh=mesh, in_specs=placed, out_specs=P("ctx", "tp"), check_vma=False
    )
```

```python
import functools

import jax
import jax.numpy as jnp
from jax import lax
from jax.experimental import pallas as pl
from jax.experimental.pallas import tpu as pltpu
from jax.sharding import PartitionSpec as P

HEAD_DIM = 128
MOST = 4096


NEGATIVE = -1e30
ROPE_BASE = 500000.0
EPSILON = 1e-05


def doc_starts(doc_lengths):
    ends = jnp.cumsum(doc_lengths)
    return ends - doc_lengths


def seg_info(positions, starts):
    inside = starts[None, :] <= positions[:, None]
    segment = jnp.sum(inside.astype(jnp.int32), axis=1) - 1
    doc_first = jnp.max(jnp.where(inside, starts[None, :], 0), axis=1)
    return (segment, doc_first)


def rotate(lifted, offsets):
    halfway = lifted.shape[-1] // 2
    fraction = jnp.arange(halfway, dtype=jnp.float32) * (2.0 / lifted.shape[-1])
    inverse = jnp.exp(-jnp.log(jnp.float32(ROPE_BASE)) * fraction)
    angles = offsets.astype(jnp.float32)[:, None] * inverse[None, :]
    cosine = jnp.cos(angles)[:, None, :]
    sine_table = jnp.sin(angles)[:, None, :]
    leading = lifted[..., :halfway]
    trailing = lifted[..., halfway:]
    return jnp.concatenate(
        [leading * cosine - trailing * sine_table, trailing * cosine + leading * sine_table],
        axis=-1,
    )


def normalize(tokens, norm_gain):
    widened = tokens.astype(jnp.float32)
    square = jnp.mean(widened * widened, axis=-1, keepdims=True)
    return (widened * lax.rsqrt(square + EPSILON) * norm_gain.astype(jnp.float32)).astype(
        jnp.bfloat16
    )


def project(normed, weight, offsets):
    head_count = weight.shape[1] // HEAD_DIM
    lifted = jnp.dot(normed, weight, preferred_element_type=jnp.float32)
    lifted = lifted.reshape(normed.shape[0], head_count, HEAD_DIM)
    return rotate(lifted, offsets).astype(jnp.bfloat16)


def flash_kernel(bounds, kinds, picks, q_ref, kseg_ref, qseg_ref, *rest, heads):
    o_ref, kv_ref, m_sc, l_sc, acc_sc = rest[-5:]
    part_refs = rest[:-5]
    step = pl.program_id(0)
    first = bounds[0]
    own = bounds[1]
    block = first + step
    rows = q_ref.shape[0]
    kind = kinds[step]

    @pl.when(step == 0)
    def _():
        m_sc[...] = jnp.full(m_sc.shape, NEGATIVE, jnp.float32)
        l_sc[...] = jnp.zeros(l_sc.shape, jnp.float32)
        acc_sc[...] = jnp.zeros(acc_sc.shape, jnp.float32)

    for index, part in enumerate(part_refs):

        @pl.when((kind > 0) & (picks[step] == index))
        def _():
            kv_ref[...] = part[...]

    def absorb(masked):
        keys = kv_ref[0]
        values = jnp.concatenate([kv_ref[1], jnp.ones((rows, HEAD_DIM), jnp.bfloat16)], axis=1)
        if masked:
            query_places = own * rows + lax.broadcasted_iota(jnp.int32, (rows, rows), 0)
            key_places = block * rows + lax.broadcasted_iota(jnp.int32, (rows, rows), 1)
            allowed = (qseg_ref[...] == kseg_ref[...]) & (key_places <= query_places)
        for h in range(heads):
            query = q_ref[:, h * HEAD_DIM:(h + 1) * HEAD_DIM]
            scores = lax.dot_general(
                query, keys, (((1,), (1,)), ((), ())), preferred_element_type=jnp.float32
            ) * HEAD_DIM ** (-0.5)
            if masked:
                scores = jnp.where(allowed, scores, NEGATIVE)
            highest = jnp.max(scores, axis=1, keepdims=True)
            raised = jnp.exp(scores - highest)
            if masked:
                raised = jnp.where(allowed, raised, 0.0)
            both = jnp.dot(raised.astype(jnp.bfloat16), values, preferred_element_type=jnp.float32)
            numerator = both[:, :HEAD_DIM]
            denominator = both[:, HEAD_DIM:]
            previous = m_sc[h]
            summit = jnp.maximum(previous, highest)
            retain = jnp.exp(previous - summit)
            admit = jnp.exp(highest - summit)
            acc_sc[h] = acc_sc[h] * retain + numerator * admit
            l_sc[h] = l_sc[h] * retain + denominator * admit
            m_sc[h] = summit

    @pl.when(kind == 1)
    def _():
        absorb(False)

    @pl.when(kind == 2)
    def _():
        absorb(True)

    @pl.when(step == pl.num_programs(0) - 1)
    def _():
        for h in range(heads):
            o_ref[:, h * HEAD_DIM:(h + 1) * HEAD_DIM] = (acc_sc[h] / l_sc[h]).astype(o_ref.dtype)


def flash(bounds, kinds, picks, queries, parts, key_segments, query_segments, steps):
    rows, width = queries.shape
    heads = width // HEAD_DIM

    def kseg_map(step, b, k, p):
        return (0, jnp.minimum(b[0] + step, b[1]))

    def whole(step, b, k, p):
        return (0, 0, 0)

    grid_spec = pltpu.PrefetchScalarGridSpec(
        num_scalar_prefetch=3,
        grid=(steps,),
        in_specs=[
            pl.BlockSpec((rows, width), lambda step, b, k, p: (0, 0)),
            pl.BlockSpec((1, rows), kseg_map),
            pl.BlockSpec((rows, 1), lambda step, b, k, p: (0, 0)),
        ]
        + [pl.BlockSpec(part.shape, whole) for part in parts],
        out_specs=pl.BlockSpec((rows, width), lambda step, b, k, p: (0, 0)),
        scratch_shapes=[
            pltpu.VMEM(parts[0].shape, parts[0].dtype),
            pltpu.VMEM((heads, rows, HEAD_DIM), jnp.float32),
            pltpu.VMEM((heads, rows, HEAD_DIM), jnp.float32),
            pltpu.VMEM((heads, rows, HEAD_DIM), jnp.float32),
        ],
    )
    return pl.pallas_call(
        functools.partial(flash_kernel, heads=heads),
        grid_spec=grid_spec,
        out_shape=jax.ShapeDtypeStruct((rows, width), jnp.bfloat16),
    )(bounds, kinds, picks, queries, key_segments, query_segments, *parts)


def steps_needed(shard_rows, ctx_count):
    return min(ctx_count, -(-(MOST - 1) // shard_rows) + 1)


def earlier_blocks(packed, axis, span):
    count = lax.axis_size(axis)
    reach = span // 2
    chain = [packed]
    for k in range(1, reach + 1):
        pairs = [(i, i + 2 * k) for i in range(count - 2 * k)]
        chain.append(lax.ppermute(packed, axis, pairs))
    sibling = lax.ppermute(tuple(chain), axis, [(i, i ^ 1) for i in range(count)])
    return chain + list(sibling)


def part_of(offset, place, reach):
    sibling_index = reach + 1 + (offset + 1 - 2 * (place % 2)) // 2
    return jnp.where(offset % 2 == 0, offset // 2, sibling_index)


def on_device(tokens, doc_lengths, norm_gain, w_query, w_key, w_value, w_out):
    shard_rows = tokens.shape[0]
    ctx_count = lax.axis_size("ctx")
    ctx_place = lax.axis_index("ctx")
    starts = doc_starts(doc_lengths)
    local_places = jnp.arange(shard_rows, dtype=jnp.int32)
    positions = ctx_place * shard_rows + local_places
    segment, doc_first = seg_info(positions, starts)
    every_place = jnp.arange(shard_rows * ctx_count, dtype=jnp.int32)
    every_segment, unused_first = seg_info(every_place, starts)
    normed = normalize(tokens, norm_gain)
    offsets = positions - doc_first
    queries = project(normed, w_query, offsets).reshape(shard_rows, -1)
    keys = project(normed, w_key, offsets).reshape(shard_rows, -1)
    values = jnp.dot(normed, w_value, preferred_element_type=jnp.float32).astype(jnp.bfloat16)
    packed = jnp.stack([keys, values])
    gathered = earlier_blocks(packed, "ctx", steps_needed(shard_rows, ctx_count))
    bounds = jnp.stack([doc_first[0] // shard_rows, ctx_place]).astype(jnp.int32)
    steps = steps_needed(shard_rows, ctx_count)
    visited = bounds[0] + jnp.arange(steps, dtype=jnp.int32)
    head_segment = every_segment[jnp.minimum(visited, ctx_place) * shard_rows]
    whole = (visited < ctx_place) & (head_segment == segment[shard_rows - 1])
    kinds = jnp.where(visited > ctx_place, 0, jnp.where(whole, 1, 2)).astype(jnp.int32)
    offsets_back = ctx_place - jnp.minimum(visited, ctx_place)
    picks = part_of(offsets_back, ctx_place, steps // 2).astype(jnp.int32)
    attended = flash(
        bounds,
        kinds,
        picks,
        queries,
        gathered,
        every_segment.reshape(1, -1).astype(jnp.int32),
        segment.reshape(-1, 1).astype(jnp.int32),
        steps,
    )
    return scatter_sum(attended, w_out, "tp")


def scatter_sum(attended, w_out, axis):
    count = lax.axis_size(axis)
    place = lax.axis_index(axis)
    width = w_out.shape[1] // count
    rightward = [(i, (i + 1) % count) for i in range(count)]
    leftward = [(i, (i - 1) % count) for i in range(count)]

    products = jnp.einsum(
        "tk,kjc->jtc",
        attended,
        w_out.reshape(w_out.shape[0], count, width),
        preferred_element_type=jnp.float32,
    ).astype(jnp.bfloat16)

    def pick(index):
        chunk = lax.dynamic_index_in_dim(products, index % count, axis=0, keepdims=False)
        return chunk.astype(jnp.float32)

    reach_right = count // 2
    reach_left = count - 1 - reach_right
    from_left = pick(place + reach_right)
    from_right = pick(place - reach_left)
    for hop in range(1, reach_right + 1):
        from_left = lax.ppermute(from_left.astype(jnp.bfloat16), axis, rightward).astype(jnp.float32)
        if hop <= reach_left:
            from_right = lax.ppermute(from_right.astype(jnp.bfloat16), axis, leftward).astype(
                jnp.float32
            )
        if hop < reach_right:
            from_left = from_left + pick(place + reach_right - hop)
        if hop < reach_left:
            from_right = from_right + pick(place - reach_left + hop)
    return (from_left + from_right + pick(place)).astype(jnp.bfloat16)


def solution(mesh):
    placed = (P("ctx", None), P(), P(), P(None, "tp"), P(None, "tp"), P(None, "tp"), P("tp", None))
    return jax.shard_map(
        on_device, mesh=mesh, in_specs=placed, out_specs=P("ctx", "tp"), check_vma=False
    )
```

```python
import functools

import jax
import jax.numpy as jnp
from jax import lax
from jax.experimental import pallas as pl
from jax.experimental.pallas import tpu as pltpu
from jax.sharding import PartitionSpec as P

HEAD_DIM = 128
MOST = 4096


NEGATIVE = -1e30
ROPE_BASE = 500000.0
EPSILON = 1e-05


def doc_starts(doc_lengths):
    ends = jnp.cumsum(doc_lengths)
    return ends - doc_lengths


def seg_info(positions, starts):
    inside = starts[None, :] <= positions[:, None]
    segment = jnp.sum(inside.astype(jnp.int32), axis=1) - 1
    doc_first = jnp.max(jnp.where(inside, starts[None, :], 0), axis=1)
    return (segment, doc_first)


def rotate(lifted, offsets):
    halfway = lifted.shape[-1] // 2
    fraction = jnp.arange(halfway, dtype=jnp.float32) * (2.0 / lifted.shape[-1])
    inverse = jnp.exp(-jnp.log(jnp.float32(ROPE_BASE)) * fraction)
    angles = offsets.astype(jnp.float32)[:, None] * inverse[None, :]
    cosine = jnp.cos(angles)[:, None, :]
    sine_table = jnp.sin(angles)[:, None, :]
    leading = lifted[..., :halfway]
    trailing = lifted[..., halfway:]
    return jnp.concatenate(
        [leading * cosine - trailing * sine_table, trailing * cosine + leading * sine_table],
        axis=-1,
    )


def normalize(tokens, norm_gain):
    widened = tokens.astype(jnp.float32)
    square = jnp.mean(widened * widened, axis=-1, keepdims=True)
    return (widened * lax.rsqrt(square + EPSILON) * norm_gain.astype(jnp.float32)).astype(
        jnp.bfloat16
    )


def project(normed, weight, offsets):
    head_count = weight.shape[1] // HEAD_DIM
    lifted = jnp.dot(normed, weight, preferred_element_type=jnp.float32)
    lifted = lifted.reshape(normed.shape[0], head_count, HEAD_DIM)
    return rotate(lifted, offsets).astype(jnp.bfloat16)


def flash_kernel(bounds, kinds, picks, q_ref, qfirst_ref, *rest, heads):
    o_ref, kv_ref, m_sc, l_sc, acc_sc = rest[-5:]
    part_refs = rest[:-5]
    step = pl.program_id(0)
    first = bounds[0]
    own = bounds[1]
    block = first + step
    rows = q_ref.shape[0]
    kind = kinds[step]

    @pl.when(step == 0)
    def _():
        m_sc[...] = jnp.full(m_sc.shape, NEGATIVE, jnp.float32)
        l_sc[...] = jnp.zeros(l_sc.shape, jnp.float32)
        acc_sc[...] = jnp.zeros(acc_sc.shape, jnp.float32)

    for index, part in enumerate(part_refs):

        @pl.when((kind > 0) & (picks[step] == index))
        def _():
            kv_ref[...] = part[...]

    def absorb(masked):
        keys = kv_ref[0]
        values = jnp.concatenate([kv_ref[1], jnp.ones((rows, HEAD_DIM), jnp.bfloat16)], axis=1)
        if masked:
            query_places = own * rows + lax.broadcasted_iota(jnp.int32, (rows, rows), 0)
            key_places = block * rows + lax.broadcasted_iota(jnp.int32, (rows, rows), 1)
            allowed = (key_places >= qfirst_ref[...]) & (key_places <= query_places)
        for h in range(heads):
            query = q_ref[:, h * HEAD_DIM:(h + 1) * HEAD_DIM]
            scores = lax.dot_general(
                query, keys, (((1,), (1,)), ((), ())), preferred_element_type=jnp.float32
            ) * HEAD_DIM ** (-0.5)
            if masked:
                scores = jnp.where(allowed, scores, NEGATIVE)
            highest = jnp.max(scores, axis=1, keepdims=True)
            raised = jnp.exp(scores - highest)
            if masked:
                raised = jnp.where(allowed, raised, 0.0)
            both = jnp.dot(raised.astype(jnp.bfloat16), values, preferred_element_type=jnp.float32)
            numerator = both[:, :HEAD_DIM]
            denominator = both[:, HEAD_DIM:]
            previous = m_sc[h]
            summit = jnp.maximum(previous, highest)
            retain = jnp.exp(previous - summit)
            admit = jnp.exp(highest - summit)
            acc_sc[h] = acc_sc[h] * retain + numerator * admit
            l_sc[h] = l_sc[h] * retain + denominator * admit
            m_sc[h] = summit

    @pl.when(kind == 1)
    def _():
        absorb(False)

    @pl.when(kind == 2)
    def _():
        absorb(True)

    @pl.when(step == pl.num_programs(0) - 1)
    def _():
        for h in range(heads):
            o_ref[:, h * HEAD_DIM:(h + 1) * HEAD_DIM] = (acc_sc[h] / l_sc[h]).astype(o_ref.dtype)


def flash(bounds, kinds, picks, queries, parts, query_firsts, steps):
    rows, width = queries.shape
    heads = width // HEAD_DIM

    def whole(step, b, k, p):
        return (0, 0, 0)

    grid_spec = pltpu.PrefetchScalarGridSpec(
        num_scalar_prefetch=3,
        grid=(steps,),
        in_specs=[
            pl.BlockSpec((rows, width), lambda step, b, k, p: (0, 0)),
            pl.BlockSpec((rows, 1), lambda step, b, k, p: (0, 0)),
        ]
        + [pl.BlockSpec(part.shape, whole) for part in parts],
        out_specs=pl.BlockSpec((rows, width), lambda step, b, k, p: (0, 0)),
        scratch_shapes=[
            pltpu.VMEM(parts[0].shape, parts[0].dtype),
            pltpu.VMEM((heads, rows, HEAD_DIM), jnp.float32),
            pltpu.VMEM((heads, rows, HEAD_DIM), jnp.float32),
            pltpu.VMEM((heads, rows, HEAD_DIM), jnp.float32),
        ],
    )
    return pl.pallas_call(
        functools.partial(flash_kernel, heads=heads),
        grid_spec=grid_spec,
        out_shape=jax.ShapeDtypeStruct((rows, width), jnp.bfloat16),
    )(bounds, kinds, picks, queries, query_firsts, *parts)


def steps_needed(shard_rows, ctx_count):
    return min(ctx_count, -(-(MOST - 1) // shard_rows) + 1)


def earlier_blocks(packed, axis, span):
    count = lax.axis_size(axis)
    reach = span // 2
    chain = [packed]
    for k in range(1, reach + 1):
        pairs = [(i, i + 2 * k) for i in range(count - 2 * k)]
        chain.append(lax.ppermute(packed, axis, pairs))
    sibling = lax.ppermute(tuple(chain), axis, [(i, i ^ 1) for i in range(count)])
    return chain + list(sibling)


def part_of(offset, place, reach):
    sibling_index = reach + 1 + (offset + 1 - 2 * (place % 2)) // 2
    return jnp.where(offset % 2 == 0, offset // 2, sibling_index)


def on_device(tokens, doc_lengths, norm_gain, w_query, w_key, w_value, w_out):
    shard_rows = tokens.shape[0]
    ctx_count = lax.axis_size("ctx")
    ctx_place = lax.axis_index("ctx")
    starts = doc_starts(doc_lengths)
    local_places = jnp.arange(shard_rows, dtype=jnp.int32)
    positions = ctx_place * shard_rows + local_places
    segment, doc_first = seg_info(positions, starts)
    normed = normalize(tokens, norm_gain)
    offsets = positions - doc_first
    queries = project(normed, w_query, offsets).reshape(shard_rows, -1)
    keys = project(normed, w_key, offsets).reshape(shard_rows, -1)
    values = jnp.dot(normed, w_value, preferred_element_type=jnp.float32).astype(jnp.bfloat16)
    packed = jnp.stack([keys, values])
    gathered = earlier_blocks(packed, "ctx", steps_needed(shard_rows, ctx_count))
    bounds = jnp.stack([doc_first[0] // shard_rows, ctx_place]).astype(jnp.int32)
    steps = steps_needed(shard_rows, ctx_count)
    visited = bounds[0] + jnp.arange(steps, dtype=jnp.int32)
    whole = (visited < ctx_place) & (visited * shard_rows >= doc_first[shard_rows - 1])
    kinds = jnp.where(visited > ctx_place, 0, jnp.where(whole, 1, 2)).astype(jnp.int32)
    offsets_back = ctx_place - jnp.minimum(visited, ctx_place)
    picks = part_of(offsets_back, ctx_place, steps // 2).astype(jnp.int32)
    attended = flash(
        bounds,
        kinds,
        picks,
        queries,
        gathered,
        doc_first.reshape(-1, 1).astype(jnp.int32),
        steps,
    )
    return scatter_sum(attended, w_out, "tp")


def scatter_sum(attended, w_out, axis):
    count = lax.axis_size(axis)
    place = lax.axis_index(axis)
    width = w_out.shape[1] // count
    rightward = [(i, (i + 1) % count) for i in range(count)]
    leftward = [(i, (i - 1) % count) for i in range(count)]

    def pick(index):
        columns = lax.dynamic_slice_in_dim(w_out, (index % count) * width, width, axis=1)
        partial_value = jnp.dot(attended, columns, preferred_element_type=jnp.float32)
        return partial_value.astype(jnp.bfloat16).astype(jnp.float32)

    reach_right = count // 2
    reach_left = count - 1 - reach_right
    from_left = pick(place + reach_right)
    from_right = pick(place - reach_left)
    for hop in range(1, reach_right + 1):
        from_left = lax.ppermute(from_left.astype(jnp.bfloat16), axis, rightward).astype(jnp.float32)
        if hop <= reach_left:
            from_right = lax.ppermute(from_right.astype(jnp.bfloat16), axis, leftward).astype(
                jnp.float32
            )
        if hop < reach_right:
            from_left = from_left + pick(place + reach_right - hop)
        if hop < reach_left:
            from_right = from_right + pick(place - reach_left + hop)
    return (from_left + from_right + pick(place)).astype(jnp.bfloat16)


def solution(mesh):
    placed = (P("ctx", None), P(), P(), P(None, "tp"), P(None, "tp"), P(None, "tp"), P("tp", None))
    return jax.shard_map(
        on_device, mesh=mesh, in_specs=placed, out_specs=P("ctx", "tp"), check_vma=False
    )
```

```python
import functools

import jax
import jax.numpy as jnp
from jax import lax
from jax.experimental import pallas as pl
from jax.experimental.pallas import tpu as pltpu
from jax.sharding import PartitionSpec as P

HEAD_DIM = 128
MOST = 4096


NEGATIVE = -1e30
ROPE_BASE = 500000.0
EPSILON = 1e-05


def doc_starts(doc_lengths):
    ends = jnp.cumsum(doc_lengths)
    return ends - doc_lengths


def seg_info(positions, starts):
    inside = starts[None, :] <= positions[:, None]
    segment = jnp.sum(inside.astype(jnp.int32), axis=1) - 1
    doc_first = jnp.max(jnp.where(inside, starts[None, :], 0), axis=1)
    return (segment, doc_first)


def rotate(lifted, offsets):
    halfway = lifted.shape[-1] // 2
    fraction = jnp.arange(halfway, dtype=jnp.float32) * (2.0 / lifted.shape[-1])
    inverse = jnp.exp(-jnp.log(jnp.float32(ROPE_BASE)) * fraction)
    angles = offsets.astype(jnp.float32)[:, None] * inverse[None, :]
    cosine = jnp.cos(angles)[:, None, :]
    sine_table = jnp.sin(angles)[:, None, :]
    leading = lifted[..., :halfway]
    trailing = lifted[..., halfway:]
    return jnp.concatenate(
        [leading * cosine - trailing * sine_table, trailing * cosine + leading * sine_table],
        axis=-1,
    )


def normalize(tokens, norm_gain):
    widened = tokens.astype(jnp.float32)
    square = jnp.mean(widened * widened, axis=-1, keepdims=True)
    return (widened * lax.rsqrt(square + EPSILON) * norm_gain.astype(jnp.float32)).astype(
        jnp.bfloat16
    )


def project(normed, weight, offsets):
    head_count = weight.shape[1] // HEAD_DIM
    lifted = jnp.dot(normed, weight, preferred_element_type=jnp.float32)
    lifted = lifted.reshape(normed.shape[0], head_count, HEAD_DIM)
    return rotate(lifted, offsets).astype(jnp.bfloat16)


def flash_kernel(own_ref, blocks, kinds, picks, q_ref, qfirst_ref, *rest, heads, parts, carry_in, carry_out):
    part_refs = rest[:parts]
    rest = rest[parts:]
    if carry_in:
        m_in, l_in, acc_in = rest[:3]
        rest = rest[3:]
    if carry_out:
        m_sc, l_sc, acc_sc, kv_ref = rest
    else:
        o_ref, kv_ref, m_sc, l_sc, acc_sc = rest
    step = pl.program_id(0)
    own = own_ref[0]
    block = blocks[step]
    rows = q_ref.shape[0]
    kind = kinds[step]

    @pl.when(step == 0)
    def _():
        if carry_in:
            m_sc[...] = m_in[...]
            l_sc[...] = l_in[...]
            acc_sc[...] = acc_in[...]
        else:
            m_sc[...] = jnp.full(m_sc.shape, NEGATIVE, jnp.float32)
            l_sc[...] = jnp.zeros(l_sc.shape, jnp.float32)
            acc_sc[...] = jnp.zeros(acc_sc.shape, jnp.float32)

    for index, part in enumerate(part_refs):

        @pl.when((kind > 0) & (picks[step] == index))
        def _():
            kv_ref[...] = part[...]

    def absorb(masked):
        keys = kv_ref[0]
        values = jnp.concatenate([kv_ref[1], jnp.ones((rows, HEAD_DIM), jnp.bfloat16)], axis=1)
        if masked:
            query_places = own * rows + lax.broadcasted_iota(jnp.int32, (rows, rows), 0)
            key_places = block * rows + lax.broadcasted_iota(jnp.int32, (rows, rows), 1)
            allowed = (key_places >= qfirst_ref[...]) & (key_places <= query_places)
        for h in range(heads):
            query = q_ref[:, h * HEAD_DIM:(h + 1) * HEAD_DIM]
            scores = lax.dot_general(
                query, keys, (((1,), (1,)), ((), ())), preferred_element_type=jnp.float32
            ) * HEAD_DIM ** (-0.5)
            if masked:
                scores = jnp.where(allowed, scores, NEGATIVE)
            highest = jnp.max(scores, axis=1, keepdims=True)
            raised = jnp.exp(scores - highest)
            if masked:
                raised = jnp.where(allowed, raised, 0.0)
            both = jnp.dot(raised.astype(jnp.bfloat16), values, preferred_element_type=jnp.float32)
            numerator = both[:, :HEAD_DIM]
            denominator = both[:, HEAD_DIM:]
            previous = m_sc[h]
            summit = jnp.maximum(previous, highest)
            retain = jnp.exp(previous - summit)
            admit = jnp.exp(highest - summit)
            acc_sc[h] = acc_sc[h] * retain + numerator * admit
            l_sc[h] = l_sc[h] * retain + denominator * admit
            m_sc[h] = summit

    @pl.when(kind == 1)
    def _():
        absorb(False)

    @pl.when(kind == 2)
    def _():
        absorb(True)

    if not carry_out:

        @pl.when(step == pl.num_programs(0) - 1)
        def _():
            for h in range(heads):
                o_ref[:, h * HEAD_DIM:(h + 1) * HEAD_DIM] = (acc_sc[h] / l_sc[h]).astype(
                    o_ref.dtype
                )


def flash(own, blocks, kinds, picks, queries, parts, query_firsts, carry):
    rows, width = queries.shape
    heads = width // HEAD_DIM
    steps = blocks.shape[0]

    def fixed(step, *prefetched):
        return (0, 0)

    def whole(step, *prefetched):
        return (0, 0, 0)

    state = jax.ShapeDtypeStruct((heads, rows, HEAD_DIM), jnp.float32)
    in_specs = [
        pl.BlockSpec((rows, width), fixed),
        pl.BlockSpec((rows, 1), fixed),
    ] + [pl.BlockSpec(part.shape, whole) for part in parts]
    operands = [queries, query_firsts] + list(parts)
    if carry is not None:
        in_specs += [pl.BlockSpec(state.shape, whole)] * 3
        operands += list(carry)
        out_shape = jax.ShapeDtypeStruct((rows, width), jnp.bfloat16)
        out_specs = pl.BlockSpec((rows, width), fixed)
        scratch = [pltpu.VMEM(parts[0].shape, parts[0].dtype)] + [pltpu.VMEM(state.shape, jnp.float32)] * 3
    else:
        out_shape = (state, state, state)
        out_specs = (pl.BlockSpec(state.shape, whole),) * 3
        scratch = [pltpu.VMEM(parts[0].shape, parts[0].dtype)]
    grid_spec = pltpu.PrefetchScalarGridSpec(
        num_scalar_prefetch=4,
        grid=(steps,),
        in_specs=in_specs,
        out_specs=out_specs,
        scratch_shapes=scratch,
    )
    kernel = functools.partial(
        flash_kernel,
        heads=heads,
        parts=len(parts),
        carry_in=carry is not None,
        carry_out=carry is None,
    )
    return pl.pallas_call(kernel, grid_spec=grid_spec, out_shape=out_shape)(
        own, blocks, kinds, picks, *operands
    )


def steps_needed(shard_rows, ctx_count):
    return min(ctx_count, -(-(MOST - 1) // shard_rows) + 1)


def earlier_blocks(packed, axis, span):
    count = lax.axis_size(axis)
    reach = span // 2
    chain = [packed]
    for k in range(1, reach + 1):
        pairs = [(i, i + 2 * k) for i in range(count - 2 * k)]
        chain.append(lax.ppermute(packed, axis, pairs))
    sibling = lax.ppermute(tuple(chain), axis, [(i, i ^ 1) for i in range(count)])
    return chain + list(sibling)


def on_device(tokens, doc_lengths, norm_gain, w_query, w_key, w_value, w_out):
    shard_rows = tokens.shape[0]
    ctx_count = lax.axis_size("ctx")
    ctx_place = lax.axis_index("ctx")
    starts = doc_starts(doc_lengths)
    local_places = jnp.arange(shard_rows, dtype=jnp.int32)
    positions = ctx_place * shard_rows + local_places
    segment, doc_first = seg_info(positions, starts)
    normed = normalize(tokens, norm_gain)
    offsets = positions - doc_first
    queries = project(normed, w_query, offsets).reshape(shard_rows, -1)
    keys = project(normed, w_key, offsets).reshape(shard_rows, -1)
    values = jnp.dot(normed, w_value, preferred_element_type=jnp.float32).astype(jnp.bfloat16)
    packed = jnp.stack([keys, values])
    gathered = earlier_blocks(packed, "ctx", steps_needed(shard_rows, ctx_count))
    bounds = jnp.stack([doc_first[0] // shard_rows, ctx_place]).astype(jnp.int32)
    steps = steps_needed(shard_rows, ctx_count)
    reach = steps // 2
    own = ctx_place.reshape(1).astype(jnp.int32)
    last_first = doc_first[shard_rows - 1]

    def plan(offsets_back):
        visited = ctx_place - offsets_back
        whole = (offsets_back > 0) & (visited * shard_rows >= last_first)
        kinds = jnp.where(visited < bounds[0], 0, jnp.where(whole, 1, 2)).astype(jnp.int32)
        return jnp.maximum(visited, 0).astype(jnp.int32), kinds

    near_offsets = 2 * jnp.arange(reach + 1, dtype=jnp.int32)
    near_blocks, near_kinds = plan(near_offsets)
    near_picks = jnp.arange(reach + 1, dtype=jnp.int32)
    far_offsets = 2 * jnp.arange(reach, dtype=jnp.int32) + 1
    far_blocks, far_kinds = plan(far_offsets)
    far_picks = (far_offsets + 1 - 2 * (ctx_place % 2)) // 2
    query_firsts = doc_first.reshape(-1, 1).astype(jnp.int32)
    carry = flash(
        own, near_blocks, near_kinds, near_picks, queries, gathered[:reach + 1], query_firsts, None
    )
    attended = flash(
        own,
        far_blocks,
        far_kinds,
        far_picks.astype(jnp.int32),
        queries,
        gathered[reach + 1:],
        query_firsts,
        carry,
    )
    return scatter_sum(attended, w_out, "tp")


def scatter_sum(attended, w_out, axis):
    count = lax.axis_size(axis)
    place = lax.axis_index(axis)
    width = w_out.shape[1] // count
    rightward = [(i, (i + 1) % count) for i in range(count)]
    leftward = [(i, (i - 1) % count) for i in range(count)]

    def pick(index):
        columns = lax.dynamic_slice_in_dim(w_out, (index % count) * width, width, axis=1)
        partial_value = jnp.dot(attended, columns, preferred_element_type=jnp.float32)
        return partial_value.astype(jnp.bfloat16).astype(jnp.float32)

    reach_right = count // 2
    reach_left = count - 1 - reach_right
    from_left = pick(place + reach_right)
    from_right = pick(place - reach_left)
    for hop in range(1, reach_right + 1):
        from_left = lax.ppermute(from_left.astype(jnp.bfloat16), axis, rightward).astype(jnp.float32)
        if hop <= reach_left:
            from_right = lax.ppermute(from_right.astype(jnp.bfloat16), axis, leftward).astype(
                jnp.float32
            )
        if hop < reach_right:
            from_left = from_left + pick(place + reach_right - hop)
        if hop < reach_left:
            from_right = from_right + pick(place - reach_left + hop)
    return (from_left + from_right + pick(place)).astype(jnp.bfloat16)


def solution(mesh):
    placed = (P("ctx", None), P(), P(), P(None, "tp"), P(None, "tp"), P(None, "tp"), P("tp", None))
    return jax.shard_map(
        on_device, mesh=mesh, in_specs=placed, out_specs=P("ctx", "tp"), check_vma=False
    )
```

```python
import functools

import jax
import jax.numpy as jnp
from jax import lax
from jax.experimental import pallas as pl
from jax.experimental.pallas import tpu as pltpu
from jax.sharding import PartitionSpec as P

HEAD_DIM = 128
MOST = 4096


NEGATIVE = -1e30
ROPE_BASE = 500000.0
EPSILON = 1e-05


def doc_starts(doc_lengths):
    ends = jnp.cumsum(doc_lengths)
    return ends - doc_lengths


def seg_info(positions, starts):
    inside = starts[None, :] <= positions[:, None]
    segment = jnp.sum(inside.astype(jnp.int32), axis=1) - 1
    doc_first = jnp.max(jnp.where(inside, starts[None, :], 0), axis=1)
    return (segment, doc_first)


def rotate(lifted, offsets):
    halfway = lifted.shape[-1] // 2
    fraction = jnp.arange(halfway, dtype=jnp.float32) * (2.0 / lifted.shape[-1])
    inverse = jnp.exp(-jnp.log(jnp.float32(ROPE_BASE)) * fraction)
    angles = offsets.astype(jnp.float32)[:, None] * inverse[None, :]
    cosine = jnp.cos(angles)[:, None, :]
    sine_table = jnp.sin(angles)[:, None, :]
    leading = lifted[..., :halfway]
    trailing = lifted[..., halfway:]
    return jnp.concatenate(
        [leading * cosine - trailing * sine_table, trailing * cosine + leading * sine_table],
        axis=-1,
    )


def normalize(tokens, norm_gain):
    widened = tokens.astype(jnp.float32)
    square = jnp.mean(widened * widened, axis=-1, keepdims=True)
    return (widened * lax.rsqrt(square + EPSILON) * norm_gain.astype(jnp.float32)).astype(
        jnp.bfloat16
    )


def project(normed, weight, offsets):
    head_count = weight.shape[1] // HEAD_DIM
    lifted = jnp.dot(normed, weight, preferred_element_type=jnp.float32)
    lifted = lifted.reshape(normed.shape[0], head_count, HEAD_DIM)
    return rotate(lifted, offsets).astype(jnp.bfloat16)


def flash_kernel(bounds, kinds, picks, q_ref, qfirst_ref, *rest, heads):
    o_ref, kv_ref, m_sc, l_sc, acc_sc = rest[-5:]
    part_refs = rest[:-5]
    step = pl.program_id(0)
    first = bounds[0]
    own = bounds[1]
    block = first + step
    rows = q_ref.shape[0]
    kind = kinds[step]

    @pl.when(step == 0)
    def _():
        m_sc[...] = jnp.full(m_sc.shape, NEGATIVE, jnp.float32)
        l_sc[...] = jnp.zeros(l_sc.shape, jnp.float32)
        acc_sc[...] = jnp.zeros(acc_sc.shape, jnp.float32)

    for index, part in enumerate(part_refs):

        @pl.when((kind > 0) & (picks[step] == index))
        def _():
            kv_ref[...] = part[...]

    def absorb(masked):
        keys = kv_ref[0]
        values = jnp.concatenate([kv_ref[1], jnp.ones((rows, HEAD_DIM), jnp.bfloat16)], axis=1)
        if masked:
            query_places = own * rows + lax.broadcasted_iota(jnp.int32, (rows, rows), 0)
            key_places = block * rows + lax.broadcasted_iota(jnp.int32, (rows, rows), 1)
            allowed = (key_places >= qfirst_ref[...]) & (key_places <= query_places)
        for h in range(heads):
            query = q_ref[:, h * HEAD_DIM:(h + 1) * HEAD_DIM]
            scores = lax.dot_general(
                query, keys, (((1,), (1,)), ((), ())), preferred_element_type=jnp.float32
            ) * HEAD_DIM ** (-0.5)
            if masked:
                scores = jnp.where(allowed, scores, NEGATIVE)
            highest = jnp.max(scores, axis=1, keepdims=True)
            raised = jnp.exp(scores - highest)
            if masked:
                raised = jnp.where(allowed, raised, 0.0)
            both = jnp.dot(raised.astype(jnp.bfloat16), values, preferred_element_type=jnp.float32)
            numerator = both[:, :HEAD_DIM]
            denominator = both[:, HEAD_DIM:]
            previous = m_sc[h]
            summit = jnp.maximum(previous, highest)
            retain = jnp.exp(previous - summit)
            admit = jnp.exp(highest - summit)
            acc_sc[h] = acc_sc[h] * retain + numerator * admit
            l_sc[h] = l_sc[h] * retain + denominator * admit
            m_sc[h] = summit

    @pl.when(kind == 1)
    def _():
        absorb(False)

    @pl.when(kind == 2)
    def _():
        absorb(True)

    @pl.when(step == pl.num_programs(0) - 1)
    def _():
        for h in range(heads):
            o_ref[:, h * HEAD_DIM:(h + 1) * HEAD_DIM] = (acc_sc[h] / l_sc[h]).astype(o_ref.dtype)


def flash(bounds, kinds, picks, queries, parts, query_firsts, steps):
    rows, width = queries.shape
    heads = width // HEAD_DIM

    def whole(step, b, k, p):
        return (0, 0, 0)

    grid_spec = pltpu.PrefetchScalarGridSpec(
        num_scalar_prefetch=3,
        grid=(steps,),
        in_specs=[
            pl.BlockSpec((rows, width), lambda step, b, k, p: (0, 0)),
            pl.BlockSpec((rows, 1), lambda step, b, k, p: (0, 0)),
        ]
        + [pl.BlockSpec(part.shape, whole) for part in parts],
        out_specs=pl.BlockSpec((rows, width), lambda step, b, k, p: (0, 0)),
        scratch_shapes=[
            pltpu.VMEM(parts[0].shape, parts[0].dtype),
            pltpu.VMEM((heads, rows, HEAD_DIM), jnp.float32),
            pltpu.VMEM((heads, rows, HEAD_DIM), jnp.float32),
            pltpu.VMEM((heads, rows, HEAD_DIM), jnp.float32),
        ],
    )
    return pl.pallas_call(
        functools.partial(flash_kernel, heads=heads),
        grid_spec=grid_spec,
        out_shape=jax.ShapeDtypeStruct((rows, width), jnp.bfloat16),
    )(bounds, kinds, picks, queries, query_firsts, *parts)


def steps_needed(shard_rows, ctx_count):
    return min(ctx_count, -(-(MOST - 1) // shard_rows) + 1)


def earlier_blocks(packed, axis, span):
    count = lax.axis_size(axis)
    reach = span // 2
    chain = [packed]
    for k in range(1, reach + 1):
        pairs = [(i, i + 2 * k) for i in range(count - 2 * k)]
        chain.append(lax.ppermute(packed, axis, pairs))
    sibling = lax.ppermute(tuple(chain), axis, [(i, i ^ 1) for i in range(count)])
    return chain + list(sibling)


def part_of(offset, place, reach):
    sibling_index = reach + 1 + (offset + 1 - 2 * (place % 2)) // 2
    return jnp.where(offset % 2 == 0, offset // 2, sibling_index)


def on_device(tokens, doc_lengths, norm_gain, w_query, w_key, w_value, w_out):
    shard_rows = tokens.shape[0]
    ctx_count = lax.axis_size("ctx")
    ctx_place = lax.axis_index("ctx")
    starts = doc_starts(doc_lengths)
    local_places = jnp.arange(shard_rows, dtype=jnp.int32)
    positions = ctx_place * shard_rows + local_places
    segment, doc_first = seg_info(positions, starts)
    normed = normalize(tokens, norm_gain)
    offsets = positions - doc_first
    queries = project(normed, w_query, offsets).reshape(shard_rows, -1)
    keys = project(normed, w_key, offsets).reshape(shard_rows, -1)
    values = jnp.dot(normed, w_value, preferred_element_type=jnp.float32).astype(jnp.bfloat16)
    packed = jnp.stack([keys, values])
    gathered = earlier_blocks(packed, "ctx", steps_needed(shard_rows, ctx_count))
    bounds = jnp.stack([doc_first[0] // shard_rows, ctx_place]).astype(jnp.int32)
    steps = steps_needed(shard_rows, ctx_count)
    visited = bounds[0] + jnp.arange(steps, dtype=jnp.int32)
    whole = (visited < ctx_place) & (visited * shard_rows >= doc_first[shard_rows - 1])
    kinds = jnp.where(visited > ctx_place, 0, jnp.where(whole, 1, 2)).astype(jnp.int32)
    offsets_back = ctx_place - jnp.minimum(visited, ctx_place)
    picks = part_of(offsets_back, ctx_place, steps // 2).astype(jnp.int32)
    attended = flash(
        bounds,
        kinds,
        picks,
        queries,
        gathered,
        doc_first.reshape(-1, 1).astype(jnp.int32),
        steps,
    )
    return scatter_sum(attended, w_out, "tp")


def scatter_sum(attended, w_out, axis):
    count = lax.axis_size(axis)
    place = lax.axis_index(axis)
    width = w_out.shape[1] // count
    rightward = [(i, (i + 1) % count) for i in range(count)]
    leftward = [(i, (i - 1) % count) for i in range(count)]

    def pick(index):
        columns = lax.dynamic_slice_in_dim(w_out, (index % count) * width, width, axis=1)
        partial_value = jnp.dot(attended, columns, preferred_element_type=jnp.float32)
        return lax.optimization_barrier(partial_value.astype(jnp.bfloat16)).astype(jnp.float32)

    reach_right = count // 2
    reach_left = count - 1 - reach_right
    from_left = pick(place + reach_right)
    from_right = pick(place - reach_left)
    for hop in range(1, reach_right + 1):
        from_left = lax.ppermute(from_left.astype(jnp.bfloat16), axis, rightward).astype(jnp.float32)
        if hop <= reach_left:
            from_right = lax.ppermute(from_right.astype(jnp.bfloat16), axis, leftward).astype(
                jnp.float32
            )
        if hop < reach_right:
            from_left = from_left + pick(place + reach_right - hop)
        if hop < reach_left:
            from_right = from_right + pick(place - reach_left + hop)
    return (from_left + from_right + pick(place)).astype(jnp.bfloat16)


def solution(mesh):
    placed = (P("ctx", None), P(), P(), P(None, "tp"), P(None, "tp"), P(None, "tp"), P("tp", None))
    return jax.shard_map(
        on_device, mesh=mesh, in_specs=placed, out_specs=P("ctx", "tp"), check_vma=False
    )
```

```python
import functools

import jax
import jax.numpy as jnp
from jax import lax
from jax.experimental import pallas as pl
from jax.experimental.pallas import tpu as pltpu
from jax.sharding import PartitionSpec as P

HEAD_DIM = 128
MOST = 4096


NEGATIVE = -1e30
ROPE_BASE = 500000.0
EPSILON = 1e-05


def doc_starts(doc_lengths):
    ends = jnp.cumsum(doc_lengths)
    return ends - doc_lengths


def seg_info(positions, starts):
    inside = starts[None, :] <= positions[:, None]
    segment = jnp.sum(inside.astype(jnp.int32), axis=1) - 1
    doc_first = jnp.max(jnp.where(inside, starts[None, :], 0), axis=1)
    return (segment, doc_first)


def rotate(lifted, offsets):
    halfway = lifted.shape[-1] // 2
    fraction = jnp.arange(halfway, dtype=jnp.float32) * (2.0 / lifted.shape[-1])
    inverse = jnp.exp(-jnp.log(jnp.float32(ROPE_BASE)) * fraction)
    angles = offsets.astype(jnp.float32)[:, None] * inverse[None, :]
    cosine = jnp.cos(angles)[:, None, :]
    sine_table = jnp.sin(angles)[:, None, :]
    leading = lifted[..., :halfway]
    trailing = lifted[..., halfway:]
    return jnp.concatenate(
        [leading * cosine - trailing * sine_table, trailing * cosine + leading * sine_table],
        axis=-1,
    )


def normalize(tokens, norm_gain):
    widened = tokens.astype(jnp.float32)
    square = jnp.mean(widened * widened, axis=-1, keepdims=True)
    return (widened * lax.rsqrt(square + EPSILON) * norm_gain.astype(jnp.float32)).astype(
        jnp.bfloat16
    )


def project(normed, weight, offsets):
    head_count = weight.shape[1] // HEAD_DIM
    lifted = jnp.dot(normed, weight, preferred_element_type=jnp.float32)
    lifted = lifted.reshape(normed.shape[0], head_count, HEAD_DIM)
    return rotate(lifted, offsets).astype(jnp.bfloat16)


def flash_kernel(bounds, kinds, picks, q_ref, qfirst_ref, *rest, heads):
    o_ref, kv_ref, m_sc, l_sc, acc_sc = rest[-5:]
    part_refs = rest[:-5]
    step = pl.program_id(0)
    first = bounds[0]
    own = bounds[1]
    block = first + step
    rows = q_ref.shape[0]
    kind = kinds[step]

    @pl.when(step == 0)
    def _():
        m_sc[...] = jnp.full(m_sc.shape, NEGATIVE, jnp.float32)
        l_sc[...] = jnp.zeros(l_sc.shape, jnp.float32)
        acc_sc[...] = jnp.zeros(acc_sc.shape, jnp.float32)

    for index, part in enumerate(part_refs):

        @pl.when((kind > 0) & (picks[step] == index))
        def _():
            kv_ref[...] = part[...]

    def absorb(masked):
        keys = kv_ref[0]
        values = jnp.concatenate([kv_ref[1], jnp.ones((rows, HEAD_DIM), jnp.bfloat16)], axis=1)
        if masked:
            query_places = own * rows + lax.broadcasted_iota(jnp.int32, (rows, rows), 0)
            key_places = block * rows + lax.broadcasted_iota(jnp.int32, (rows, rows), 1)
            allowed = (key_places >= qfirst_ref[...]) & (key_places <= query_places)
        for h in range(heads):
            query = q_ref[:, h * HEAD_DIM:(h + 1) * HEAD_DIM]
            scores = lax.dot_general(
                query, keys, (((1,), (1,)), ((), ())), preferred_element_type=jnp.float32
            ) * HEAD_DIM ** (-0.5)
            if masked:
                scores = jnp.where(allowed, scores, NEGATIVE)
            highest = jnp.max(scores, axis=1, keepdims=True)
            raised = jnp.exp(scores - highest)
            if masked:
                raised = jnp.where(allowed, raised, 0.0)
            both = jnp.dot(raised.astype(jnp.bfloat16), values, preferred_element_type=jnp.float32)
            numerator = both[:, :HEAD_DIM]
            denominator = both[:, HEAD_DIM:]
            previous = m_sc[h]
            summit = jnp.maximum(previous, highest)
            retain = jnp.exp(previous - summit)
            admit = jnp.exp(highest - summit)
            acc_sc[h] = acc_sc[h] * retain + numerator * admit
            l_sc[h] = l_sc[h] * retain + denominator * admit
            m_sc[h] = summit

    @pl.when(kind == 1)
    def _():
        absorb(False)

    @pl.when(kind == 2)
    def _():
        absorb(True)

    @pl.when(step == pl.num_programs(0) - 1)
    def _():
        for h in range(heads):
            o_ref[:, h * HEAD_DIM:(h + 1) * HEAD_DIM] = (acc_sc[h] / l_sc[h]).astype(o_ref.dtype)


def flash(bounds, kinds, picks, queries, parts, query_firsts, steps):
    rows, width = queries.shape
    heads = width // HEAD_DIM

    def whole(step, b, k, p):
        return (0, 0, 0)

    grid_spec = pltpu.PrefetchScalarGridSpec(
        num_scalar_prefetch=3,
        grid=(steps,),
        in_specs=[
            pl.BlockSpec((rows, width), lambda step, b, k, p: (0, 0)),
            pl.BlockSpec((rows, 1), lambda step, b, k, p: (0, 0)),
        ]
        + [pl.BlockSpec(part.shape, whole) for part in parts],
        out_specs=pl.BlockSpec((rows, width), lambda step, b, k, p: (0, 0)),
        scratch_shapes=[
            pltpu.VMEM(parts[0].shape, parts[0].dtype),
            pltpu.VMEM((heads, rows, HEAD_DIM), jnp.float32),
            pltpu.VMEM((heads, rows, HEAD_DIM), jnp.float32),
            pltpu.VMEM((heads, rows, HEAD_DIM), jnp.float32),
        ],
    )
    return pl.pallas_call(
        functools.partial(flash_kernel, heads=heads),
        grid_spec=grid_spec,
        out_shape=jax.ShapeDtypeStruct((rows, width), jnp.bfloat16),
    )(bounds, kinds, picks, queries, query_firsts, *parts)


def steps_needed(shard_rows, ctx_count):
    return min(ctx_count, -(-(MOST - 1) // shard_rows) + 1)


def earlier_blocks(packed, axis, span):
    count = lax.axis_size(axis)
    reach = span // 2
    chain = [packed]
    for k in range(1, reach + 1):
        pairs = [(i, i + 2 * k) for i in range(count - 2 * k)]
        chain.append(lax.ppermute(packed, axis, pairs))
    sibling = lax.ppermute(tuple(chain), axis, [(i, i ^ 1) for i in range(count)])
    return chain + list(sibling)


def part_of(offset, place, reach):
    sibling_index = reach + 1 + (offset + 1 - 2 * (place % 2)) // 2
    return jnp.where(offset % 2 == 0, offset // 2, sibling_index)


def on_device(tokens, doc_lengths, norm_gain, w_query, w_key, w_value, w_out):
    shard_rows = tokens.shape[0]
    ctx_count = lax.axis_size("ctx")
    ctx_place = lax.axis_index("ctx")
    starts = doc_starts(doc_lengths)
    local_places = jnp.arange(shard_rows, dtype=jnp.int32)
    positions = ctx_place * shard_rows + local_places
    segment, doc_first = seg_info(positions, starts)
    normed = normalize(tokens, norm_gain)
    offsets = positions - doc_first
    queries = project(normed, w_query, offsets).reshape(shard_rows, -1)
    keys = project(normed, w_key, offsets).reshape(shard_rows, -1)
    values = jnp.dot(normed, w_value, preferred_element_type=jnp.float32).astype(jnp.bfloat16)
    packed = jnp.stack([keys, values])
    gathered = earlier_blocks(packed, "ctx", steps_needed(shard_rows, ctx_count))
    bounds = jnp.stack([doc_first[0] // shard_rows, ctx_place]).astype(jnp.int32)
    steps = steps_needed(shard_rows, ctx_count)
    visited = bounds[0] + jnp.arange(steps, dtype=jnp.int32)
    whole = (visited < ctx_place) & (visited * shard_rows >= doc_first[shard_rows - 1])
    kinds = jnp.where(visited > ctx_place, 0, jnp.where(whole, 1, 2)).astype(jnp.int32)
    offsets_back = ctx_place - jnp.minimum(visited, ctx_place)
    picks = part_of(offsets_back, ctx_place, steps // 2).astype(jnp.int32)
    attended = flash(
        bounds,
        kinds,
        picks,
        queries,
        gathered,
        doc_first.reshape(-1, 1).astype(jnp.int32),
        steps,
    )
    return scatter_sum(attended, w_out, "tp")


def scatter_sum(attended, w_out, axis):
    count = lax.axis_size(axis)
    place = lax.axis_index(axis)
    width = w_out.shape[1] // count
    rightward = [(i, (i + 1) % count) for i in range(count)]
    leftward = [(i, (i - 1) % count) for i in range(count)]
    products = jnp.einsum(
        "tk,kjc->jtc",
        attended,
        w_out.reshape(w_out.shape[0], count, width),
        preferred_element_type=jnp.float32,
    ).astype(jnp.bfloat16)
    reach_right = count // 2
    reach_left = count - 1 - reach_right
    right_order = (place + reach_right - jnp.arange(reach_right, dtype=jnp.int32)) % count
    left_order = (place - reach_left + jnp.arange(reach_left + 1, dtype=jnp.int32)) % count
    right_chunks = lax.optimization_barrier(jnp.take(products, right_order, axis=0))
    left_chunks = lax.optimization_barrier(jnp.take(products, left_order, axis=0))
    from_left = right_chunks[0].astype(jnp.float32)
    from_right = left_chunks[0].astype(jnp.float32)
    for hop in range(1, reach_right + 1):
        from_left = lax.ppermute(from_left.astype(jnp.bfloat16), axis, rightward).astype(jnp.float32)
        if hop <= reach_left:
            from_right = lax.ppermute(from_right.astype(jnp.bfloat16), axis, leftward).astype(
                jnp.float32
            )
        if hop < reach_right:
            from_left = from_left + right_chunks[hop].astype(jnp.float32)
        if hop < reach_left:
            from_right = from_right + left_chunks[hop].astype(jnp.float32)
    own_chunk = left_chunks[reach_left].astype(jnp.float32)
    return (from_left + from_right + own_chunk).astype(jnp.bfloat16)


def solution(mesh):
    placed = (P("ctx", None), P(), P(), P(None, "tp"), P(None, "tp"), P(None, "tp"), P("tp", None))
    return jax.shard_map(
        on_device, mesh=mesh, in_specs=placed, out_specs=P("ctx", "tp"), check_vma=False
    )
```

```python
import functools

import jax
import jax.numpy as jnp
from jax import lax
from jax.experimental import pallas as pl
from jax.experimental.pallas import tpu as pltpu
from jax.sharding import PartitionSpec as P

HEAD_DIM = 128
MOST = 4096
PER_STEP = 2


NEGATIVE = -1e30
ROPE_BASE = 500000.0
EPSILON = 1e-05


def doc_starts(doc_lengths):
    ends = jnp.cumsum(doc_lengths)
    return ends - doc_lengths


def seg_info(positions, starts):
    inside = starts[None, :] <= positions[:, None]
    segment = jnp.sum(inside.astype(jnp.int32), axis=1) - 1
    doc_first = jnp.max(jnp.where(inside, starts[None, :], 0), axis=1)
    return (segment, doc_first)


def rotate(lifted, offsets):
    halfway = lifted.shape[-1] // 2
    fraction = jnp.arange(halfway, dtype=jnp.float32) * (2.0 / lifted.shape[-1])
    inverse = jnp.exp(-jnp.log(jnp.float32(ROPE_BASE)) * fraction)
    angles = offsets.astype(jnp.float32)[:, None] * inverse[None, :]
    cosine = jnp.cos(angles)[:, None, :]
    sine_table = jnp.sin(angles)[:, None, :]
    leading = lifted[..., :halfway]
    trailing = lifted[..., halfway:]
    return jnp.concatenate(
        [leading * cosine - trailing * sine_table, trailing * cosine + leading * sine_table],
        axis=-1,
    )


def normalize(tokens, norm_gain):
    widened = tokens.astype(jnp.float32)
    square = jnp.mean(widened * widened, axis=-1, keepdims=True)
    return (widened * lax.rsqrt(square + EPSILON) * norm_gain.astype(jnp.float32)).astype(
        jnp.bfloat16
    )


def project(normed, weight, offsets):
    head_count = weight.shape[1] // HEAD_DIM
    lifted = jnp.dot(normed, weight, preferred_element_type=jnp.float32)
    lifted = lifted.reshape(normed.shape[0], head_count, HEAD_DIM)
    return rotate(lifted, offsets).astype(jnp.bfloat16)


def flash_kernel(bounds, kinds, picks, q_ref, qfirst_ref, *rest, heads):
    o_ref, kv_ref, m_sc, l_sc, acc_sc = rest[-5:]
    part_refs = rest[:-5]
    step = pl.program_id(0)
    first = bounds[0]
    own = bounds[1]
    rows = q_ref.shape[0]

    @pl.when(step == 0)
    def _():
        m_sc[...] = jnp.full(m_sc.shape, NEGATIVE, jnp.float32)
        l_sc[...] = jnp.zeros(l_sc.shape, jnp.float32)
        acc_sc[...] = jnp.zeros(acc_sc.shape, jnp.float32)

    def absorb(masked, block):
        keys = kv_ref[0]
        values = jnp.concatenate([kv_ref[1], jnp.ones((rows, HEAD_DIM), jnp.bfloat16)], axis=1)
        if masked:
            query_places = own * rows + lax.broadcasted_iota(jnp.int32, (rows, rows), 0)
            key_places = block * rows + lax.broadcasted_iota(jnp.int32, (rows, rows), 1)
            allowed = (key_places >= qfirst_ref[...]) & (key_places <= query_places)
        for h in range(heads):
            query = q_ref[:, h * HEAD_DIM:(h + 1) * HEAD_DIM]
            scores = lax.dot_general(
                query, keys, (((1,), (1,)), ((), ())), preferred_element_type=jnp.float32
            ) * HEAD_DIM ** (-0.5)
            if masked:
                scores = jnp.where(allowed, scores, NEGATIVE)
            highest = jnp.max(scores, axis=1, keepdims=True)
            raised = jnp.exp(scores - highest)
            if masked:
                raised = jnp.where(allowed, raised, 0.0)
            both = jnp.dot(raised.astype(jnp.bfloat16), values, preferred_element_type=jnp.float32)
            numerator = both[:, :HEAD_DIM]
            denominator = both[:, HEAD_DIM:]
            previous = m_sc[h]
            summit = jnp.maximum(previous, highest)
            retain = jnp.exp(previous - summit)
            admit = jnp.exp(highest - summit)
            acc_sc[h] = acc_sc[h] * retain + numerator * admit
            l_sc[h] = l_sc[h] * retain + denominator * admit
            m_sc[h] = summit

    for within in range(PER_STEP):
        visit = step * PER_STEP + within
        kind = kinds[visit]
        block = first + visit
        for index, part in enumerate(part_refs):

            @pl.when((kind > 0) & (picks[visit] == index))
            def _():
                kv_ref[...] = part[...]

        @pl.when(kind == 1)
        def _():
            absorb(False, block)

        @pl.when(kind == 2)
        def _():
            absorb(True, block)

    @pl.when(step == pl.num_programs(0) - 1)
    def _():
        for h in range(heads):
            o_ref[:, h * HEAD_DIM:(h + 1) * HEAD_DIM] = (acc_sc[h] / l_sc[h]).astype(o_ref.dtype)


def flash(bounds, kinds, picks, queries, parts, query_firsts, steps):
    rows, width = queries.shape
    heads = width // HEAD_DIM

    def whole(step, b, k, p):
        return (0, 0, 0)

    grid_spec = pltpu.PrefetchScalarGridSpec(
        num_scalar_prefetch=3,
        grid=(-(-steps // PER_STEP),),
        in_specs=[
            pl.BlockSpec((rows, width), lambda step, b, k, p: (0, 0)),
            pl.BlockSpec((rows, 1), lambda step, b, k, p: (0, 0)),
        ]
        + [pl.BlockSpec(part.shape, whole) for part in parts],
        out_specs=pl.BlockSpec((rows, width), lambda step, b, k, p: (0, 0)),
        scratch_shapes=[
            pltpu.VMEM(parts[0].shape, parts[0].dtype),
            pltpu.VMEM((heads, rows, HEAD_DIM), jnp.float32),
            pltpu.VMEM((heads, rows, HEAD_DIM), jnp.float32),
            pltpu.VMEM((heads, rows, HEAD_DIM), jnp.float32),
        ],
    )
    return pl.pallas_call(
        functools.partial(flash_kernel, heads=heads),
        grid_spec=grid_spec,
        out_shape=jax.ShapeDtypeStruct((rows, width), jnp.bfloat16),
    )(bounds, kinds, picks, queries, query_firsts, *parts)


def steps_needed(shard_rows, ctx_count):
    return min(ctx_count, -(-(MOST - 1) // shard_rows) + 1)


def earlier_blocks(packed, axis, span):
    count = lax.axis_size(axis)
    reach = span // 2
    chain = [packed]
    for k in range(1, reach + 1):
        pairs = [(i, i + 2 * k) for i in range(count - 2 * k)]
        chain.append(lax.ppermute(packed, axis, pairs))
    sibling = lax.ppermute(tuple(chain), axis, [(i, i ^ 1) for i in range(count)])
    return chain + list(sibling)


def part_of(offset, place, reach):
    sibling_index = reach + 1 + (offset + 1 - 2 * (place % 2)) // 2
    return jnp.where(offset % 2 == 0, offset // 2, sibling_index)


def on_device(tokens, doc_lengths, norm_gain, w_query, w_key, w_value, w_out):
    shard_rows = tokens.shape[0]
    ctx_count = lax.axis_size("ctx")
    ctx_place = lax.axis_index("ctx")
    starts = doc_starts(doc_lengths)
    local_places = jnp.arange(shard_rows, dtype=jnp.int32)
    positions = ctx_place * shard_rows + local_places
    segment, doc_first = seg_info(positions, starts)
    normed = normalize(tokens, norm_gain)
    offsets = positions - doc_first
    queries = project(normed, w_query, offsets).reshape(shard_rows, -1)
    keys = project(normed, w_key, offsets).reshape(shard_rows, -1)
    values = jnp.dot(normed, w_value, preferred_element_type=jnp.float32).astype(jnp.bfloat16)
    packed = jnp.stack([keys, values])
    gathered = earlier_blocks(packed, "ctx", steps_needed(shard_rows, ctx_count))
    bounds = jnp.stack([doc_first[0] // shard_rows, ctx_place]).astype(jnp.int32)
    steps = steps_needed(shard_rows, ctx_count)
    visited = bounds[0] + jnp.arange(-(-steps // PER_STEP) * PER_STEP, dtype=jnp.int32)
    whole = (visited < ctx_place) & (visited * shard_rows >= doc_first[shard_rows - 1])
    kinds = jnp.where(visited > ctx_place, 0, jnp.where(whole, 1, 2)).astype(jnp.int32)
    offsets_back = ctx_place - jnp.minimum(visited, ctx_place)
    picks = part_of(offsets_back, ctx_place, steps // 2).astype(jnp.int32)
    attended = flash(
        bounds,
        kinds,
        picks,
        queries,
        gathered,
        doc_first.reshape(-1, 1).astype(jnp.int32),
        steps,
    )
    return scatter_sum(attended, w_out, "tp")


def scatter_sum(attended, w_out, axis):
    count = lax.axis_size(axis)
    place = lax.axis_index(axis)
    width = w_out.shape[1] // count
    rightward = [(i, (i + 1) % count) for i in range(count)]
    leftward = [(i, (i - 1) % count) for i in range(count)]

    def pick(index):
        columns = lax.dynamic_slice_in_dim(w_out, (index % count) * width, width, axis=1)
        partial_value = jnp.dot(attended, columns, preferred_element_type=jnp.float32)
        return lax.optimization_barrier(partial_value.astype(jnp.bfloat16)).astype(jnp.float32)

    reach_right = count // 2
    reach_left = count - 1 - reach_right
    from_left = pick(place + reach_right)
    from_right = pick(place - reach_left)
    for hop in range(1, reach_right + 1):
        from_left = lax.ppermute(from_left.astype(jnp.bfloat16), axis, rightward).astype(jnp.float32)
        if hop <= reach_left:
            from_right = lax.ppermute(from_right.astype(jnp.bfloat16), axis, leftward).astype(
                jnp.float32
            )
        if hop < reach_right:
            from_left = from_left + pick(place + reach_right - hop)
        if hop < reach_left:
            from_right = from_right + pick(place - reach_left + hop)
    return (from_left + from_right + pick(place)).astype(jnp.bfloat16)


def solution(mesh):
    placed = (P("ctx", None), P(), P(), P(None, "tp"), P(None, "tp"), P(None, "tp"), P("tp", None))
    return jax.shard_map(
        on_device, mesh=mesh, in_specs=placed, out_specs=P("ctx", "tp"), check_vma=False
    )
```

```python
import functools

import jax
import jax.numpy as jnp
from jax import lax
from jax.experimental import pallas as pl
from jax.experimental.pallas import tpu as pltpu
from jax.sharding import PartitionSpec as P

HEAD_DIM = 128
MOST = 4096


NEGATIVE = -1e30
ROPE_BASE = 500000.0
EPSILON = 1e-05


def doc_starts(doc_lengths):
    ends = jnp.cumsum(doc_lengths)
    return ends - doc_lengths


def seg_info(positions, starts):
    inside = starts[None, :] <= positions[:, None]
    segment = jnp.sum(inside.astype(jnp.int32), axis=1) - 1
    doc_first = jnp.max(jnp.where(inside, starts[None, :], 0), axis=1)
    return (segment, doc_first)


def rotate(lifted, offsets):
    halfway = lifted.shape[-1] // 2
    fraction = jnp.arange(halfway, dtype=jnp.float32) * (2.0 / lifted.shape[-1])
    inverse = jnp.exp(-jnp.log(jnp.float32(ROPE_BASE)) * fraction)
    angles = offsets.astype(jnp.float32)[:, None] * inverse[None, :]
    cosine = jnp.cos(angles)[:, None, :]
    sine_table = jnp.sin(angles)[:, None, :]
    leading = lifted[..., :halfway]
    trailing = lifted[..., halfway:]
    return jnp.concatenate(
        [leading * cosine - trailing * sine_table, trailing * cosine + leading * sine_table],
        axis=-1,
    )


def normalize(tokens, norm_gain):
    widened = tokens.astype(jnp.float32)
    square = jnp.mean(widened * widened, axis=-1, keepdims=True)
    return (widened * lax.rsqrt(square + EPSILON) * norm_gain.astype(jnp.float32)).astype(
        jnp.bfloat16
    )


def project(normed, weight, offsets):
    head_count = weight.shape[1] // HEAD_DIM
    lifted = jnp.dot(normed, weight, preferred_element_type=jnp.float32)
    lifted = lifted.reshape(normed.shape[0], head_count, HEAD_DIM)
    return rotate(lifted, offsets).astype(jnp.bfloat16)


def flash_kernel(bounds, kinds, picks, q_ref, qfirst_ref, *rest, heads):
    o_ref, kv_ref, m_sc, l_sc, acc_sc = rest[-5:]
    part_refs = rest[:-5]
    step = pl.program_id(0)
    first = bounds[0]
    own = bounds[1]
    block = first + step
    rows = q_ref.shape[0]
    kind = kinds[step]

    @pl.when(step == 0)
    def _():
        m_sc[...] = jnp.full(m_sc.shape, NEGATIVE, jnp.float32)
        l_sc[...] = jnp.zeros(l_sc.shape, jnp.float32)
        acc_sc[...] = jnp.zeros(acc_sc.shape, jnp.float32)

    for index, part in enumerate(part_refs):

        @pl.when((kind > 0) & (picks[step] == index))
        def _():
            kv_ref[...] = part[...]

    def absorb(masked):
        keys = kv_ref[0]
        values = jnp.concatenate([kv_ref[1], jnp.ones((rows, HEAD_DIM), jnp.bfloat16)], axis=1)
        if masked:
            query_places = own * rows + lax.broadcasted_iota(jnp.int32, (rows, rows), 0)
            key_places = block * rows + lax.broadcasted_iota(jnp.int32, (rows, rows), 1)
            allowed = (key_places >= qfirst_ref[...]) & (key_places <= query_places)
        for h in range(heads):
            query = q_ref[:, h * HEAD_DIM:(h + 1) * HEAD_DIM]
            scores = lax.dot_general(
                query, keys, (((1,), (1,)), ((), ())), preferred_element_type=jnp.float32
            ) * HEAD_DIM ** (-0.5)
            if masked:
                scores = jnp.where(allowed, scores, NEGATIVE)
            highest = jnp.max(scores, axis=1, keepdims=True)
            raised = jnp.exp(scores - highest)
            if masked:
                raised = jnp.where(allowed, raised, 0.0)
            both = jnp.dot(raised.astype(jnp.bfloat16), values, preferred_element_type=jnp.float32)
            numerator = both[:, :HEAD_DIM]
            denominator = both[:, HEAD_DIM:]
            previous = m_sc[h]
            summit = jnp.maximum(previous, highest)
            retain = jnp.exp(previous - summit)
            admit = jnp.exp(highest - summit)
            acc_sc[h] = acc_sc[h] * retain + numerator * admit
            l_sc[h] = l_sc[h] * retain + denominator * admit
            m_sc[h] = summit

    @pl.when(kind == 1)
    def _():
        absorb(False)

    @pl.when(kind == 2)
    def _():
        absorb(True)

    @pl.when(step == pl.num_programs(0) - 1)
    def _():
        for h in range(heads):
            o_ref[:, h * HEAD_DIM:(h + 1) * HEAD_DIM] = (acc_sc[h] / l_sc[h]).astype(o_ref.dtype)


def flash(bounds, kinds, picks, queries, parts, query_firsts, steps):
    rows, width = queries.shape
    heads = width // HEAD_DIM

    def whole(step, b, k, p):
        return (0, 0, 0)

    grid_spec = pltpu.PrefetchScalarGridSpec(
        num_scalar_prefetch=3,
        grid=(steps,),
        in_specs=[
            pl.BlockSpec((rows, width), lambda step, b, k, p: (0, 0)),
            pl.BlockSpec((rows, 1), lambda step, b, k, p: (0, 0)),
        ]
        + [pl.BlockSpec(part.shape, whole) for part in parts],
        out_specs=pl.BlockSpec((rows, width), lambda step, b, k, p: (0, 0)),
        scratch_shapes=[
            pltpu.VMEM(parts[0].shape, parts[0].dtype),
            pltpu.VMEM((heads, rows, HEAD_DIM), jnp.float32),
            pltpu.VMEM((heads, rows, HEAD_DIM), jnp.float32),
            pltpu.VMEM((heads, rows, HEAD_DIM), jnp.float32),
        ],
    )
    return pl.pallas_call(
        functools.partial(flash_kernel, heads=heads),
        grid_spec=grid_spec,
        out_shape=jax.ShapeDtypeStruct((rows, width), jnp.bfloat16),
    )(bounds, kinds, picks, queries, query_firsts, *parts)


def steps_needed(shard_rows, ctx_count):
    return min(ctx_count, -(-(MOST - 1) // shard_rows) + 1)


def earlier_blocks(packed, axis, span):
    count = lax.axis_size(axis)
    reach = span // 2
    chain = [packed]
    for k in range(1, reach + 1):
        pairs = [(i, i + 2 * k) for i in range(count - 2 * k)]
        chain.append(lax.ppermute(packed, axis, pairs))
    sibling = lax.ppermute(tuple(chain), axis, [(i, i ^ 1) for i in range(count)])
    return chain + list(sibling)


def part_of(offset, place, reach):
    sibling_index = reach + 1 + (offset + 1 - 2 * (place % 2)) // 2
    return jnp.where(offset % 2 == 0, offset // 2, sibling_index)


def on_device(tokens, doc_lengths, norm_gain, w_query, w_key, w_value, w_out):
    shard_rows = tokens.shape[0]
    ctx_count = lax.axis_size("ctx")
    ctx_place = lax.axis_index("ctx")
    starts = doc_starts(doc_lengths)
    local_places = jnp.arange(shard_rows, dtype=jnp.int32)
    positions = ctx_place * shard_rows + local_places
    segment, doc_first = seg_info(positions, starts)
    normed = normalize(tokens, norm_gain)
    offsets = positions - doc_first
    queries = project(normed, w_query, offsets).reshape(shard_rows, -1)
    keys = project(normed, w_key, offsets).reshape(shard_rows, -1)
    values = jnp.dot(normed, w_value, preferred_element_type=jnp.float32).astype(jnp.bfloat16)
    packed = jnp.stack([keys, values])
    gathered = earlier_blocks(packed, "ctx", steps_needed(shard_rows, ctx_count))
    bounds = jnp.stack([doc_first[0] // shard_rows, ctx_place]).astype(jnp.int32)
    steps = steps_needed(shard_rows, ctx_count)
    visited = bounds[0] + jnp.arange(steps, dtype=jnp.int32)
    whole = (visited < ctx_place) & (visited * shard_rows >= doc_first[shard_rows - 1])
    kinds = jnp.where(visited > ctx_place, 0, jnp.where(whole, 1, 2)).astype(jnp.int32)
    offsets_back = ctx_place - jnp.minimum(visited, ctx_place)
    picks = part_of(offsets_back, ctx_place, steps // 2).astype(jnp.int32)
    attended = flash(
        bounds,
        kinds,
        picks,
        queries,
        gathered,
        doc_first.reshape(-1, 1).astype(jnp.int32),
        steps,
    )
    return scatter_sum(attended, w_out, "tp")


def scatter_sum(attended, w_out, axis):
    count = lax.axis_size(axis)
    place = lax.axis_index(axis)
    width = w_out.shape[1] // count
    rightward = [(i, (i + 1) % count) for i in range(count)]
    leftward = [(i, (i - 1) % count) for i in range(count)]

    by_chunk = jnp.transpose(w_out.reshape(w_out.shape[0], count, width), (1, 0, 2))

    def pick(index):
        columns = lax.dynamic_index_in_dim(by_chunk, index % count, axis=0, keepdims=False)
        partial_value = jnp.dot(attended, columns, preferred_element_type=jnp.float32)
        return lax.optimization_barrier(partial_value.astype(jnp.bfloat16)).astype(jnp.float32)

    reach_right = count // 2
    reach_left = count - 1 - reach_right
    from_left = pick(place + reach_right)
    from_right = pick(place - reach_left)
    for hop in range(1, reach_right + 1):
        from_left = lax.ppermute(from_left.astype(jnp.bfloat16), axis, rightward).astype(jnp.float32)
        if hop <= reach_left:
            from_right = lax.ppermute(from_right.astype(jnp.bfloat16), axis, leftward).astype(
                jnp.float32
            )
        if hop < reach_right:
            from_left = from_left + pick(place + reach_right - hop)
        if hop < reach_left:
            from_right = from_right + pick(place - reach_left + hop)
    return (from_left + from_right + pick(place)).astype(jnp.bfloat16)


def solution(mesh):
    placed = (P("ctx", None), P(), P(), P(None, "tp"), P(None, "tp"), P(None, "tp"), P("tp", None))
    return jax.shard_map(
        on_device, mesh=mesh, in_specs=placed, out_specs=P("ctx", "tp"), check_vma=False
    )
```

```python
import functools

import jax
import jax.numpy as jnp
from jax import lax
from jax.experimental import pallas as pl
from jax.experimental.pallas import tpu as pltpu
from jax.sharding import PartitionSpec as P

HEAD_DIM = 128
MOST = 4096


NEGATIVE = -1e30
ROPE_BASE = 500000.0
EPSILON = 1e-05


def doc_starts(doc_lengths):
    ends = jnp.cumsum(doc_lengths)
    return ends - doc_lengths


def seg_info(positions, starts):
    inside = starts[None, :] <= positions[:, None]
    segment = jnp.sum(inside.astype(jnp.int32), axis=1) - 1
    doc_first = jnp.max(jnp.where(inside, starts[None, :], 0), axis=1)
    return (segment, doc_first)


def rotate(lifted, offsets):
    halfway = lifted.shape[-1] // 2
    fraction = jnp.arange(halfway, dtype=jnp.float32) * (2.0 / lifted.shape[-1])
    inverse = jnp.exp(-jnp.log(jnp.float32(ROPE_BASE)) * fraction)
    angles = offsets.astype(jnp.float32)[:, None] * inverse[None, :]
    cosine = jnp.cos(angles)[:, None, :]
    sine_table = jnp.sin(angles)[:, None, :]
    leading = lifted[..., :halfway]
    trailing = lifted[..., halfway:]
    return jnp.concatenate(
        [leading * cosine - trailing * sine_table, trailing * cosine + leading * sine_table],
        axis=-1,
    )


def normalize(tokens, norm_gain):
    widened = tokens.astype(jnp.float32)
    square = jnp.mean(widened * widened, axis=-1, keepdims=True)
    return (widened * lax.rsqrt(square + EPSILON) * norm_gain.astype(jnp.float32)).astype(
        jnp.bfloat16
    )


def project(normed, weight, offsets):
    head_count = weight.shape[1] // HEAD_DIM
    lifted = jnp.dot(normed, weight, preferred_element_type=jnp.float32)
    lifted = lifted.reshape(normed.shape[0], head_count, HEAD_DIM)
    return rotate(lifted, offsets).astype(jnp.bfloat16)


def flash_kernel(bounds, kinds, picks, q_ref, qfirst_ref, *rest, heads):
    o_ref, kv_ref, m_sc, l_sc, acc_sc = rest[-5:]
    part_refs = rest[:-5]
    step = pl.program_id(0)
    first = bounds[0]
    own = bounds[1]
    block = first + step
    rows = q_ref.shape[0]
    kind = kinds[step]

    @pl.when(step == 0)
    def _():
        m_sc[...] = jnp.full(m_sc.shape, NEGATIVE, jnp.float32)
        l_sc[...] = jnp.zeros(l_sc.shape, jnp.float32)
        acc_sc[...] = jnp.zeros(acc_sc.shape, jnp.float32)

    for index, part in enumerate(part_refs):

        @pl.when((kind > 0) & (picks[step] == index))
        def _():
            kv_ref[...] = part[...]

    def absorb(masked):
        keys = kv_ref[0]
        values = jnp.concatenate([kv_ref[1], jnp.ones((rows, HEAD_DIM), jnp.bfloat16)], axis=1)
        if masked:
            query_places = own * rows + lax.broadcasted_iota(jnp.int32, (rows, rows), 0)
            key_places = block * rows + lax.broadcasted_iota(jnp.int32, (rows, rows), 1)
            allowed = (key_places >= qfirst_ref[...]) & (key_places <= query_places)
        for h in range(heads):
            query = q_ref[:, h * HEAD_DIM:(h + 1) * HEAD_DIM]
            scores = lax.dot_general(
                query, keys, (((1,), (1,)), ((), ())), preferred_element_type=jnp.float32
            ) * HEAD_DIM ** (-0.5)
            if masked:
                scores = jnp.where(allowed, scores, NEGATIVE)
            highest = jnp.max(scores, axis=1, keepdims=True)
            raised = jnp.exp(scores - highest)
            if masked:
                raised = jnp.where(allowed, raised, 0.0)
            both = jnp.dot(raised.astype(jnp.bfloat16), values, preferred_element_type=jnp.float32)
            numerator = both[:, :HEAD_DIM]
            denominator = both[:, HEAD_DIM:]
            previous = m_sc[h]
            summit = jnp.maximum(previous, highest)
            retain = jnp.exp(previous - summit)
            admit = jnp.exp(highest - summit)
            acc_sc[h] = acc_sc[h] * retain + numerator * admit
            l_sc[h] = l_sc[h] * retain + denominator * admit
            m_sc[h] = summit

    @pl.when(kind == 1)
    def _():
        absorb(False)

    @pl.when(kind == 2)
    def _():
        absorb(True)

    @pl.when(step == pl.num_programs(0) - 1)
    def _():
        for h in range(heads):
            o_ref[:, h * HEAD_DIM:(h + 1) * HEAD_DIM] = (acc_sc[h] / l_sc[h]).astype(o_ref.dtype)


def flash(bounds, kinds, picks, queries, parts, query_firsts, steps):
    rows, width = queries.shape
    heads = width // HEAD_DIM

    def whole(step, b, k, p):
        return (0, 0, 0)

    grid_spec = pltpu.PrefetchScalarGridSpec(
        num_scalar_prefetch=3,
        grid=(steps,),
        in_specs=[
            pl.BlockSpec((rows, width), lambda step, b, k, p: (0, 0)),
            pl.BlockSpec((rows, 1), lambda step, b, k, p: (0, 0)),
        ]
        + [pl.BlockSpec(part.shape, whole) for part in parts],
        out_specs=pl.BlockSpec((rows, width), lambda step, b, k, p: (0, 0)),
        scratch_shapes=[
            pltpu.VMEM(parts[0].shape, parts[0].dtype),
            pltpu.VMEM((heads, rows, HEAD_DIM), jnp.float32),
            pltpu.VMEM((heads, rows, HEAD_DIM), jnp.float32),
            pltpu.VMEM((heads, rows, HEAD_DIM), jnp.float32),
        ],
    )
    return pl.pallas_call(
        functools.partial(flash_kernel, heads=heads),
        grid_spec=grid_spec,
        out_shape=jax.ShapeDtypeStruct((rows, width), jnp.bfloat16),
    )(bounds, kinds, picks, queries, query_firsts, *parts)


def steps_needed(shard_rows, ctx_count):
    return min(ctx_count, -(-(MOST - 1) // shard_rows) + 1)


def earlier_blocks(packed, axis, span):
    count = lax.axis_size(axis)
    reach = span // 2
    chain = [packed]
    for k in range(1, reach + 1):
        pairs = [(i, i + 2 * k) for i in range(count - 2 * k)]
        chain.append(lax.ppermute(packed, axis, pairs))
    sibling = lax.ppermute(tuple(chain), axis, [(i, i ^ 1) for i in range(count)])
    return chain + list(sibling)


def part_of(offset, place, reach):
    sibling_index = reach + 1 + (offset + 1 - 2 * (place % 2)) // 2
    return jnp.where(offset % 2 == 0, offset // 2, sibling_index)


def on_device(tokens, doc_lengths, norm_gain, w_query, w_key, w_value, w_out):
    shard_rows = tokens.shape[0]
    ctx_count = lax.axis_size("ctx")
    ctx_place = lax.axis_index("ctx")
    starts = doc_starts(doc_lengths)
    local_places = jnp.arange(shard_rows, dtype=jnp.int32)
    positions = ctx_place * shard_rows + local_places
    segment, doc_first = seg_info(positions, starts)
    normed = normalize(tokens, norm_gain)
    offsets = positions - doc_first
    queries = project(normed, w_query, offsets).reshape(shard_rows, -1)
    keys = project(normed, w_key, offsets).reshape(shard_rows, -1)
    values = jnp.dot(normed, w_value, preferred_element_type=jnp.float32).astype(jnp.bfloat16)
    packed = jnp.stack([keys, values])
    gathered = earlier_blocks(packed, "ctx", steps_needed(shard_rows, ctx_count))
    bounds = jnp.stack([doc_first[0] // shard_rows, ctx_place]).astype(jnp.int32)
    steps = steps_needed(shard_rows, ctx_count)
    visited = bounds[0] + jnp.arange(steps, dtype=jnp.int32)
    whole = (visited < ctx_place) & (visited * shard_rows >= doc_first[shard_rows - 1])
    kinds = jnp.where(visited > ctx_place, 0, jnp.where(whole, 1, 2)).astype(jnp.int32)
    offsets_back = ctx_place - jnp.minimum(visited, ctx_place)
    picks = part_of(offsets_back, ctx_place, steps // 2).astype(jnp.int32)
    attended = flash(
        bounds,
        kinds,
        picks,
        queries,
        gathered,
        doc_first.reshape(-1, 1).astype(jnp.int32),
        steps,
    )
    return scatter_sum(attended, w_out, "tp")


def scatter_sum(attended, w_out, axis):
    count = lax.axis_size(axis)
    place = lax.axis_index(axis)
    width = w_out.shape[1] // count
    rightward = [(i, (i + 1) % count) for i in range(count)]
    leftward = [(i, (i - 1) % count) for i in range(count)]

    def pick(index):
        columns = lax.dynamic_slice_in_dim(w_out, (index % count) * width, width, axis=1)
        partial_value = jnp.dot(attended, columns, preferred_element_type=jnp.float32)
        return lax.optimization_barrier(partial_value.astype(jnp.bfloat16)).astype(jnp.float32)

    reach_right = count - 1 - count // 2
    reach_left = count // 2
    from_left = pick(place + reach_right)
    from_right = pick(place - reach_left)
    for hop in range(1, max(reach_right, reach_left) + 1):
        if hop <= reach_right:
            from_left = lax.ppermute(from_left.astype(jnp.bfloat16), axis, rightward).astype(
                jnp.float32
            )
        if hop <= reach_left:
            from_right = lax.ppermute(from_right.astype(jnp.bfloat16), axis, leftward).astype(
                jnp.float32
            )
        if hop < reach_right:
            from_left = from_left + pick(place + reach_right - hop)
        if hop < reach_left:
            from_right = from_right + pick(place - reach_left + hop)
    return (from_left + from_right + pick(place)).astype(jnp.bfloat16)


def solution(mesh):
    placed = (P("ctx", None), P(), P(), P(None, "tp"), P(None, "tp"), P(None, "tp"), P("tp", None))
    return jax.shard_map(
        on_device, mesh=mesh, in_specs=placed, out_specs=P("ctx", "tp"), check_vma=False
    )
```
